128 devices in a mesh: dp: 16 (over x, z), fsdp: 8 (over y, core).
Axes of the slice: x: 4, y: 4, z: 4, core: 2. Of those that a mesh axis runs over, the one named last changes fastest.
Arguments:
- tokens: bfloat16 [2048, 4096], P('dp', 'fsdp'), may hold values from -6 to 6
- expert_ids: int32 [2048, 2], P('dp'), may hold values from 0 to 7, all different within a row; in each aligned block of 128 rows (0 to 127, 128 to 255, ...) at most 40 rows name the same one
- route_probs: float32 [2048, 2], P('dp'), may hold values from 0.1 to 0.9
- w_gate: bfloat16 [4096, 65536], P(None, ('dp', 'fsdp')), may hold values from -0.09375 to 0.09375
- w_up: bfloat16 [4096, 65536], P(None, ('dp', 'fsdp')), may hold values from -0.09375 to 0.09375
- w_down: bfloat16 [65536, 4096], P(('dp', 'fsdp')), may hold values from -0.0625 to 0.0625
- out_grad: bfloat16 [2048, 4096], P('dp', 'fsdp'), may hold values from -0.59765625 to 0.59765625
Outputs:
- mixed: bfloat16 [2048, 4096], P('dp', 'fsdp')
- token_grad: bfloat16 [2048, 4096], P('dp', 'fsdp')
- prob_grad: float32 [2048, 2], P('dp')
- gate_weight_grad: bfloat16 [4096, 65536], P(None, ('dp', 'fsdp'))
- up_weight_grad: bfloat16 [4096, 65536], P(None, ('dp', 'fsdp'))
- down_weight_grad: bfloat16 [65536, 4096], P(('dp', 'fsdp'))
The draws below stay inside these ranges and needn't reach their ends.
Inputs may be any that keep to these rules, and one draw needn't show every extreme that they name: `expert_ids`: each token names two different experts. Within the 128 tokens of one dp index (aligned blocks of rows) no expert is named more than 40 times, and in some block one expert is named exactly 40 times.
All inputs are finite; a program needn't handle non-finite values.
Results may differ from the reference program's by a relative error of at most 0.019.
Values may be sent and summed in bfloat16 or wider, within the bound.
No kernel may reach another device: no remote copies, remote signals or barrier semaphores. Data moves between devices by JAX's collectives and lax.ppermute only.
A program may use at most 128 MiB of HBM per device.

```python
import math
import jax
import jax.numpy as jnp
import numpy as np
from jax import lax

D = 4096
E = 8
FF = 8192
TOK_DP = 128
CAP = 40
TOKENS = 2048
HID_DEV = 512
N_DP = 16


def levels(key, extent, split, smallest, top_value):
    def one(dim, shards_of):
        draws = jax.random.uniform(jax.random.fold_in(jax.random.fold_in(key, 6), dim), (shards_of,), jnp.float32, smallest / len(split), top_value / len(split))
        return jnp.repeat(jnp.exp(draws), extent[dim] // shards_of).reshape((-1,) + (1,) * (len(extent) - dim - 1))

    level = one(*split[0])
    for cut in split[1:]:
        level = level * one(*cut)
    return level


def assign_block(key, own, number, rows, amount, top, limit, skew):
    sequence = jax.random.permutation(key, amount)
    heavy_load, common = portions_of(amount, rows * top, limit, skew, True), portions_of(amount, rows * top, limit, skew, False)
    places = jnp.arange(amount)

    def named(lengths, rotation):
        used = int((lengths > 0).sum())
        fixed = max(1, used // 4)
        moved = fixed + (places - fixed + rotation * (used - fixed)) % max(1, amount - fixed)
        return jnp.zeros((amount,), jnp.int32).at[sequence[jnp.where(places < fixed, places, moved)]].set(jnp.asarray(lengths, jnp.int32))

    lengths = jnp.where(number % 4 == 0, named(heavy_load, number // 4), named(common, number - number // 4 - 1))
    mixed = jax.random.permutation(jax.random.fold_in(own, 3), amount)
    donor, receiver = mixed[0:amount // 2 * 2:2], mixed[1:amount // 2 * 2:2]
    room = jnp.minimum(lengths[donor] - 1, limit - lengths[receiver]) // 2
    room = jnp.where((donor == sequence[0]) | (receiver == sequence[0]) | (lengths[receiver] == 0), 0, jnp.maximum(room, 0))
    moved = jax.random.randint(jax.random.fold_in(own, 4), (amount // 2,), 0, 1 << 20) % (room + 1)
    lengths = lengths.at[donor].add(-moved).at[receiver].add(moved)
    labels = jnp.searchsorted(jnp.cumsum(lengths), jnp.arange(rows * top), side="right").astype(jnp.int32)
    grid = labels.reshape(top, rows).T
    grid = grid[jax.random.permutation(jax.random.fold_in(own, 1), rows)]
    rotation = jax.random.randint(jax.random.fold_in(own, 2), (rows, 1), 0, top)
    return jnp.take_along_axis(grid, (jnp.arange(top)[None, :] + rotation) % top, axis=1)


def portions_of(count, total, bound, skew, full):
    loads = [(1 << 20) // math.isqrt(grade ** skew) + 1 for grade in range(1, count + 1)]
    largest = bound if full else min(bound, max(-(-total // count), total * loads[0] // sum(loads)))
    least = 1 if total - largest >= count - 1 else 0
    given, spare = [largest] + [least] * (count - 1), total - largest - least * (count - 1)
    while spare > 0:
        free = [i for i in range(1, count) if given[i] < largest] or [i for i in range(1, count) if given[i] < bound]
        pool, remaining = sum([loads[i] for i in free]), spare
        for i in free:
            extra = min(bound - given[i], max(1, remaining * loads[i] // pool), spare)
            given[i] = given[i] + extra
            spare = spare - extra
    return np.array(given)


def normal_values(key, extent, width, most, split=(), held_as=jnp.bfloat16):
    values = jax.random.normal(key, extent, jnp.float32) * width
    if len(split) > 0:
        values = levels(key, extent, split, -0.22, 0.18) * values
    return jnp.clip(values, min=-most, max=most).astype(held_as)


def setup_inputs(seed: int = 0) -> dict:
    seeds = jax.random.split(jax.random.key(seed), 8)
    tokens = normal_values(seeds[0], (TOKENS, D), 1.0, 6.0, ((0, 16), (1, 8)))
    expert_ids_keys = jax.random.split(jax.random.fold_in(seeds[1], 1), TOKENS // TOK_DP)
    expert_ids_turns = jax.random.permutation(jax.random.fold_in(seeds[1], 3), TOKENS // TOK_DP)
    expert_ids = jax.vmap(lambda own, number: assign_block(jax.random.fold_in(seeds[1], 2), own, number, TOK_DP, E, 2, CAP, 2))(expert_ids_keys, expert_ids_turns).reshape((TOKENS, 2))
    route_probs = jnp.clip(0.1 + 0.79999997 * jax.random.uniform(seeds[2], (TOKENS, 2), jnp.float32) ** levels(seeds[2], (TOKENS, 2), ((0, 16),), -0.2, 0.2), 0.1, 0.9)
    w_gate = normal_values(seeds[3], (D, E * FF), D ** -0.5, 0.09375, ((1, 128),))
    w_up = normal_values(seeds[4], (D, E * FF), D ** -0.5, 0.09375, ((1, 128),))
    w_down = normal_values(seeds[5], (E * FF, D), FF ** -0.5, 0.0625, ((0, 128),))
    out_grad = normal_values(seeds[6], (TOKENS, D), 0.1, 0.59765625, ((0, 16), (1, 8)))
    return dict(tokens=tokens, expert_ids=expert_ids, route_probs=route_probs, w_gate=w_gate, w_up=w_up, w_down=w_down, out_grad=out_grad)


def expert_pass(operands):
    expert_rows, grad_rows, gate_w, up_w, down_w = operands
    gate_proj = jnp.dot(expert_rows, gate_w, preferred_element_type=jnp.float32)
    up_proj = jnp.dot(expert_rows, up_w, preferred_element_type=jnp.float32)
    sigmoid_gate = jax.nn.sigmoid(gate_proj)
    activated = gate_proj * sigmoid_gate
    hidden = (activated * up_proj).astype(jnp.bfloat16)
    blocks = FF // HID_DEV
    row_count = expert_rows.shape[0]
    hidden_blocks = hidden.reshape(row_count, blocks, HID_DEV).transpose(1, 0, 2)
    down_blocks = down_w.reshape(blocks, HID_DEV, D)

    def add_output(total, pieces):
        piece_hidden, piece_down = pieces
        term = jnp.dot(piece_hidden, piece_down, preferred_element_type=jnp.float32).astype(jnp.bfloat16)
        term = lax.optimization_barrier(term)
        return total + term.astype(jnp.float32), None

    outputs, unused = lax.scan(add_output, jnp.zeros((row_count, D), jnp.float32), (hidden_blocks, down_blocks))
    hidden_grad = lax.dot_general(grad_rows, down_w, (((1,), (1,)), ((), ())), preferred_element_type=jnp.float32)
    gate_grad = (hidden_grad * up_proj * sigmoid_gate * (1.0 + gate_proj * (1.0 - sigmoid_gate))).astype(jnp.bfloat16)
    up_grad = (hidden_grad * activated).astype(jnp.bfloat16)
    contract_rows = (((0,), (0,)), ((), ()))
    gate_w_grad = lax.dot_general(expert_rows, gate_grad, contract_rows, preferred_element_type=jnp.float32).astype(jnp.bfloat16)
    up_w_grad = lax.dot_general(expert_rows, up_grad, contract_rows, preferred_element_type=jnp.float32).astype(jnp.bfloat16)
    down_w_grad = lax.dot_general(hidden, grad_rows, contract_rows, preferred_element_type=jnp.float32).astype(jnp.bfloat16)
    gate_blocks = gate_w.reshape(D, blocks, HID_DEV).transpose(1, 0, 2)
    up_blocks = up_w.reshape(D, blocks, HID_DEV).transpose(1, 0, 2)
    gate_grad_blocks = gate_grad.reshape(row_count, blocks, HID_DEV).transpose(1, 0, 2)
    up_grad_blocks = up_grad.reshape(row_count, blocks, HID_DEV).transpose(1, 0, 2)
    back_dims = (((1,), (1,)), ((), ()))

    def add_input(total, pieces):
        piece_gate, piece_up, weight_gate, weight_up = pieces
        term = lax.dot_general(piece_gate, weight_gate, back_dims, preferred_element_type=jnp.float32)
        term = term + lax.dot_general(piece_up, weight_up, back_dims, preferred_element_type=jnp.float32)
        term = lax.optimization_barrier(term.astype(jnp.bfloat16))
        return total + term.astype(jnp.float32), None

    inputs_grad, unused = lax.scan(add_input, jnp.zeros((row_count, D), jnp.float32),
                                   (gate_grad_blocks, up_grad_blocks, gate_blocks, up_blocks))
    return outputs, inputs_grad, gate_w_grad, up_w_grad, down_w_grad


def reference(tokens, expert_ids, route_probs, w_gate, w_up, w_down, out_grad):
    pair_count = TOKENS * 2
    routing = expert_ids.reshape(-1).astype(jnp.int32)
    onehot = (routing[:, None] == jnp.arange(E, dtype=jnp.int32)[None, :]).astype(jnp.int32)
    position = jnp.sum((jnp.cumsum(onehot, axis=0) - onehot) * onehot, axis=1).astype(jnp.int32)
    capacity = N_DP * CAP
    slot_of = (routing * capacity + position).astype(jnp.int32)
    token_of = (jnp.arange(pair_count, dtype=jnp.int32) // 2).astype(jnp.int32)
    token_table = jnp.zeros((E * capacity,), jnp.int32).at[slot_of].set(token_of)
    live_rows = jnp.zeros((E * capacity,), jnp.float32).at[slot_of].set(1.0)
    prob_table = jnp.zeros((E * capacity,), jnp.float32).at[slot_of].set(route_probs.reshape(-1))
    expert_rows = (tokens[token_table].astype(jnp.float32) * live_rows[:, None]).astype(jnp.bfloat16)
    grad_rows = (out_grad[token_table].astype(jnp.float32) * prob_table[:, None]).astype(jnp.bfloat16)
    gate_all = w_gate.reshape(D, E, FF).transpose(1, 0, 2)
    up_all = w_up.reshape(D, E, FF).transpose(1, 0, 2)
    down_all = w_down.reshape(E, FF, D)
    outputs, inputs_grad, gate_w_grad, up_w_grad, down_w_grad = lax.map(
        expert_pass,
        (expert_rows.reshape(E, capacity, D), grad_rows.reshape(E, capacity, D), gate_all, up_all, down_all))
    out_pairs = outputs.reshape(E * capacity, D)[slot_of].reshape(TOKENS, 2, D)
    mixed = jnp.sum(route_probs[:, :, None] * out_pairs, axis=1).astype(jnp.bfloat16)
    prob_grad = jnp.sum(out_pairs * out_grad.astype(jnp.float32)[:, None, :], axis=2)
    token_grad = jnp.sum(inputs_grad.reshape(E * capacity, D)[slot_of].reshape(TOKENS, 2, D), axis=1).astype(jnp.bfloat16)
    gate_weight_grad = gate_w_grad.transpose(1, 0, 2).reshape(D, E * FF)
    up_weight_grad = up_w_grad.transpose(1, 0, 2).reshape(D, E * FF)
    down_weight_grad = down_w_grad.reshape(E * FF, D)
    return (mixed, token_grad, prob_grad, gate_weight_grad, up_weight_grad, down_weight_grad)
```

```python
import jax
import jax.numpy as jnp
from jax import lax
from jax.sharding import PartitionSpec as P

E = 8
CAP = 40


def local(tokens, expert_ids, route_probs, w_gate, w_up, w_down, out_grad):
    dp_count = lax.axis_size("dp")
    fsdp_count = lax.axis_size("fsdp")
    groups = dp_count // E
    token_count = tokens.shape[0]
    feat = tokens.shape[1]
    model = w_down.shape[1]
    hid = w_gate.shape[1]
    slot_total = E * CAP
    rows = dp_count * CAP
    routing = expert_ids.reshape(-1)
    onehot = (routing[:, None] == jnp.arange(E, dtype=jnp.int32)[None, :]).astype(jnp.int32)
    position = jnp.sum((jnp.cumsum(onehot, axis=0) - onehot) * onehot, axis=1)
    slot_of = (routing * CAP + position).reshape(token_count, 2)
    slot_index = jnp.arange(slot_total, dtype=jnp.int32)
    select_first = slot_of[:, 0:1] == slot_index[None, :]
    select_second = slot_of[:, 1:2] == slot_index[None, :]
    picker = jnp.logical_or(select_first, select_second)
    picker_bf = picker.astype(jnp.bfloat16)
    weighted = jnp.where(select_first, route_probs[:, 0:1], 0.0) + jnp.where(
        select_second, route_probs[:, 1:2], 0.0
    )
    contract_rows = (((0,), (0,)), ((), ()))
    back_dims = (((1,), (1,)), ((), ()))

    def place_rows(source, scaled):
        if scaled:
            placed = lax.dot_general(
                weighted,
                source.astype(jnp.float32),
                contract_rows,
                precision=lax.Precision.HIGHEST,
                preferred_element_type=jnp.float32,
            )
        else:
            placed = lax.dot_general(
                picker_bf, source, contract_rows, preferred_element_type=jnp.float32
            )
        placed = placed.astype(jnp.bfloat16).reshape(E, CAP, source.shape[1])
        return jnp.repeat(placed, groups, axis=0)

    def to_expert_layout(source, scaled):
        arrived = lax.all_to_all(
            place_rows(source, scaled), "dp", split_axis=0, concat_axis=0, tiled=True
        )
        joined = lax.all_gather(arrived.reshape(rows, feat), "fsdp", axis=0, tiled=False)
        return joined

    def to_token_layout(partial_value):
        shares = lax.psum_scatter(
            partial_value.astype(jnp.bfloat16), "fsdp", scatter_dimension=0, tiled=False
        )
        returned = lax.all_to_all(
            shares.reshape(dp_count, CAP, feat),
            "dp",
            split_axis=0,
            concat_axis=0,
            tiled=True,
        ).astype(jnp.float32)
        return jnp.sum(returned.reshape(E, groups, CAP, feat), axis=1).reshape(slot_total, feat)

    gate_w3 = w_gate.reshape(fsdp_count, feat, hid)
    up_w3 = w_up.reshape(fsdp_count, feat, hid)
    down_w3 = w_down.reshape(hid, fsdp_count, feat)
    in_dims = (((0, 2), (0, 1)), ((), ()))

    expert_rows = to_expert_layout(tokens, False)
    gate_proj = lax.dot_general(expert_rows, gate_w3, in_dims, preferred_element_type=jnp.float32)
    up_proj = lax.dot_general(expert_rows, up_w3, in_dims, preferred_element_type=jnp.float32)
    sigmoid_gate = jax.nn.sigmoid(gate_proj)
    activated = gate_proj * sigmoid_gate
    hidden = (activated * up_proj).astype(jnp.bfloat16)
    out_partial = jnp.einsum(
        "rh,hfd->frd", hidden, down_w3, preferred_element_type=jnp.float32
    )
    out_slots = to_token_layout(out_partial)
    first_pair = jnp.dot(
        select_first.astype(jnp.float32),
        out_slots,
        precision=lax.Precision.HIGHEST,
        preferred_element_type=jnp.float32,
    )
    second_pair = jnp.dot(
        select_second.astype(jnp.float32),
        out_slots,
        precision=lax.Precision.HIGHEST,
        preferred_element_type=jnp.float32,
    )
    mixed = (route_probs[:, 0:1] * first_pair + route_probs[:, 1:2] * second_pair).astype(
        jnp.bfloat16
    )
    grad_local = out_grad.astype(jnp.float32)
    prob_terms = jnp.stack(
        [jnp.sum(first_pair * grad_local, axis=1), jnp.sum(second_pair * grad_local, axis=1)],
        axis=1,
    )
    prob_grad = jnp.sum(lax.all_gather(prob_terms, "fsdp", axis=0, tiled=False), axis=0)
    grad_rows = to_expert_layout(out_grad, True)
    hidden_grad = lax.dot_general(grad_rows, down_w3, (((0, 2), (1, 2)), ((), ())),
                                  preferred_element_type=jnp.float32)
    gate_grad = (
        hidden_grad * up_proj * sigmoid_gate * (1.0 + gate_proj * (1.0 - sigmoid_gate))
    ).astype(jnp.bfloat16)
    up_grad = (hidden_grad * activated).astype(jnp.bfloat16)
    w_grad_dims = (((1,), (0,)), ((), ()))
    gate_weight_grad = lax.dot_general(
        expert_rows, gate_grad, w_grad_dims, preferred_element_type=jnp.float32
    ).astype(jnp.bfloat16).reshape(fsdp_count * feat, hid)
    up_weight_grad = lax.dot_general(
        expert_rows, up_grad, w_grad_dims, preferred_element_type=jnp.float32
    ).astype(jnp.bfloat16).reshape(fsdp_count * feat, hid)
    down_weight_grad = jnp.einsum(
        "rh,frd->hfd", hidden, grad_rows, preferred_element_type=jnp.float32
    ).astype(jnp.bfloat16).reshape(hid, model)
    input_partial = jnp.einsum(
        "rh,fdh->frd", gate_grad, gate_w3, preferred_element_type=jnp.float32
    )
    input_partial = input_partial + jnp.einsum(
        "rh,fdh->frd", up_grad, up_w3, preferred_element_type=jnp.float32
    )
    input_slots = to_token_layout(input_partial)
    token_grad = jnp.dot(
        picker.astype(jnp.float32),
        input_slots,
        precision=lax.Precision.HIGHEST,
        preferred_element_type=jnp.float32,
    ).astype(jnp.bfloat16)
    return (mixed, token_grad, prob_grad, gate_weight_grad, up_weight_grad, down_weight_grad)


def solution(mesh):
    placed = (
        P("dp", "fsdp"),
        P("dp", None),
        P("dp", None),
        P(None, ("dp", "fsdp")),
        P(None, ("dp", "fsdp")),
        P(("dp", "fsdp"), None),
        P("dp", "fsdp"),
    )
    return jax.shard_map(
        local,
        mesh=mesh,
        in_specs=placed,
        out_specs=(
            P("dp", "fsdp"),
            P("dp", "fsdp"),
            P("dp", None),
            P(None, ("dp", "fsdp")),
            P(None, ("dp", "fsdp")),
            P(("dp", "fsdp"), None),
        ),
        check_vma=False,
    )
```

```python
import jax
import jax.numpy as jnp
from jax import lax
from jax.sharding import Mesh, PartitionSpec as P

E = 8
CAP = 40


def local(tokens, expert_ids, route_probs, w_gate, w_up, w_down, out_grad):
    dp_count = lax.axis_size("dp")
    chips = lax.axis_size("fy")
    cores = lax.axis_size("fc")
    fsdp_count = chips * cores
    groups = dp_count // E
    token_count = tokens.shape[0]
    feat = tokens.shape[1]
    model = w_down.shape[1]
    hid = w_gate.shape[1]
    slot_total = E * CAP
    rows = dp_count * CAP
    core = lax.axis_index("fc")
    swap = [(0, 1), (1, 0)]
    routing = expert_ids.reshape(-1)
    onehot = (routing[:, None] == jnp.arange(E, dtype=jnp.int32)[None, :]).astype(jnp.int32)
    position = jnp.sum((jnp.cumsum(onehot, axis=0) - onehot) * onehot, axis=1)
    slot_of = (routing * CAP + position).reshape(token_count, 2)
    slot_index = jnp.arange(slot_total, dtype=jnp.int32)
    select_first = slot_of[:, 0:1] == slot_index[None, :]
    select_second = slot_of[:, 1:2] == slot_index[None, :]
    picker = jnp.logical_or(select_first, select_second)
    picker_bf = picker.astype(jnp.bfloat16)
    weighted = jnp.where(select_first, route_probs[:, 0:1], 0.0) + jnp.where(
        select_second, route_probs[:, 1:2], 0.0
    )
    contract_rows = (((0,), (0,)), ((), ()))
    back_dims = (((1,), (1,)), ((), ()))

    def place_rows(source, scaled):
        if scaled:
            placed = lax.dot_general(
                weighted,
                source.astype(jnp.float32),
                contract_rows,
                precision=lax.Precision.HIGHEST,
                preferred_element_type=jnp.float32,
            )
        else:
            placed = lax.dot_general(
                picker_bf, source, contract_rows, preferred_element_type=jnp.float32
            )
        placed = placed.astype(jnp.bfloat16).reshape(E, CAP, source.shape[1])
        return jnp.repeat(placed, groups, axis=0)

    def to_expert_layout(source, scaled):
        arrived = lax.all_to_all(
            place_rows(source, scaled), "dp", split_axis=0, concat_axis=0, tiled=True
        )
        across = lax.all_gather(arrived.reshape(rows, feat), "fy", axis=0, tiled=False)
        other = lax.ppermute(across, "fc", swap)
        joined = jnp.where(core == 0, jnp.stack([across, other], axis=1),
                           jnp.stack([other, across], axis=1))
        return joined.reshape(fsdp_count, rows, feat)

    def to_token_layout(partial_value):
        blocks = partial_value.astype(jnp.bfloat16).reshape(chips, cores, rows, feat)
        kept = lax.dynamic_index_in_dim(blocks, core, axis=1, keepdims=False)
        sent = lax.dynamic_index_in_dim(blocks, 1 - core, axis=1, keepdims=False)
        within = kept.astype(jnp.float32) + lax.ppermute(sent, "fc", swap).astype(jnp.float32)
        shares = lax.psum_scatter(within.astype(jnp.bfloat16), "fy", scatter_dimension=0, tiled=False)
        returned = lax.all_to_all(
            shares.reshape(dp_count, CAP, feat),
            "dp",
            split_axis=0,
            concat_axis=0,
            tiled=True,
        ).astype(jnp.float32)
        return jnp.sum(returned.reshape(E, groups, CAP, feat), axis=1).reshape(slot_total, feat)

    gate_w3 = w_gate.reshape(fsdp_count, feat, hid)
    up_w3 = w_up.reshape(fsdp_count, feat, hid)
    down_w3 = w_down.reshape(hid, fsdp_count, feat)
    in_dims = (((0, 2), (0, 1)), ((), ()))

    expert_rows = to_expert_layout(tokens, False)
    gate_proj = lax.dot_general(expert_rows, gate_w3, in_dims, preferred_element_type=jnp.float32)
    up_proj = lax.dot_general(expert_rows, up_w3, in_dims, preferred_element_type=jnp.float32)
    sigmoid_gate = jax.nn.sigmoid(gate_proj)
    activated = gate_proj * sigmoid_gate
    hidden = (activated * up_proj).astype(jnp.bfloat16)
    out_partial = jnp.einsum(
        "rh,hfd->frd", hidden, down_w3, preferred_element_type=jnp.float32
    )
    out_slots = to_token_layout(out_partial)
    first_pair = jnp.dot(
        select_first.astype(jnp.float32),
        out_slots,
        precision=lax.Precision.HIGHEST,
        preferred_element_type=jnp.float32,
    )
    second_pair = jnp.dot(
        select_second.astype(jnp.float32),
        out_slots,
        precision=lax.Precision.HIGHEST,
        preferred_element_type=jnp.float32,
    )
    mixed = (route_probs[:, 0:1] * first_pair + route_probs[:, 1:2] * second_pair).astype(
        jnp.bfloat16
    )
    grad_local = out_grad.astype(jnp.float32)
    prob_terms = jnp.stack(
        [jnp.sum(first_pair * grad_local, axis=1), jnp.sum(second_pair * grad_local, axis=1)],
        axis=1,
    )
    prob_grad = jnp.sum(lax.all_gather(prob_terms, ("fy", "fc"), axis=0, tiled=False), axis=0)
    grad_rows = to_expert_layout(out_grad, True)
    hidden_grad = lax.dot_general(grad_rows, down_w3, (((0, 2), (1, 2)), ((), ())),
                                  preferred_element_type=jnp.float32)
    gate_grad = (
        hidden_grad * up_proj * sigmoid_gate * (1.0 + gate_proj * (1.0 - sigmoid_gate))
    ).astype(jnp.bfloat16)
    up_grad = (hidden_grad * activated).astype(jnp.bfloat16)
    gate_weight_grad = jnp.einsum(
        "frd,rh->fdh", expert_rows, gate_grad, preferred_element_type=jnp.float32
    ).astype(jnp.bfloat16).reshape(fsdp_count * feat, hid)
    up_weight_grad = jnp.einsum(
        "frd,rh->fdh", expert_rows, up_grad, preferred_element_type=jnp.float32
    ).astype(jnp.bfloat16).reshape(fsdp_count * feat, hid)
    down_weight_grad = jnp.einsum(
        "rh,frd->hfd", hidden, grad_rows, preferred_element_type=jnp.float32
    ).astype(jnp.bfloat16).reshape(hid, model)
    input_partial = jnp.einsum(
        "rh,fdh->frd", gate_grad, gate_w3, preferred_element_type=jnp.float32
    )
    input_partial = input_partial + jnp.einsum(
        "rh,fdh->frd", up_grad, up_w3, preferred_element_type=jnp.float32
    )
    input_slots = to_token_layout(input_partial)
    token_grad = jnp.dot(
        picker.astype(jnp.float32),
        input_slots,
        precision=lax.Precision.HIGHEST,
        preferred_element_type=jnp.float32,
    ).astype(jnp.bfloat16)
    return (mixed, token_grad, prob_grad, gate_weight_grad, up_weight_grad, down_weight_grad)


def solution(mesh):
    dp_size, fsdp_size = mesh.devices.shape
    cores = 2
    split = Mesh(mesh.devices.reshape(dp_size, fsdp_size // cores, cores), ("dp", "fy", "fc"))
    fs = ("fy", "fc")
    placed = (
        P("dp", fs),
        P("dp", None),
        P("dp", None),
        P(None, ("dp",) + fs),
        P(None, ("dp",) + fs),
        P(("dp",) + fs, None),
        P("dp", fs),
    )
    return jax.shard_map(
        local,
        mesh=split,
        in_specs=placed,
        out_specs=(
            P("dp", fs),
            P("dp", fs),
            P("dp", None),
            P(None, ("dp",) + fs),
            P(None, ("dp",) + fs),
            P(("dp",) + fs, None),
        ),
        check_vma=False,
    )
```

```python
import jax
import jax.numpy as jnp
from jax import lax
from jax.sharding import Mesh, PartitionSpec as P

E = 8
CAP = 40


def local(tokens, expert_ids, route_probs, w_gate, w_up, w_down, out_grad):
    dp_count = lax.axis_size("dp")
    chips = lax.axis_size("fy")
    cores = lax.axis_size("fc")
    fsdp_count = chips * cores
    groups = dp_count // E
    token_count = tokens.shape[0]
    feat = tokens.shape[1]
    model = w_down.shape[1]
    hid = w_gate.shape[1]
    slot_total = E * CAP
    rows = dp_count * CAP
    core = lax.axis_index("fc")
    swap = [(0, 1), (1, 0)]
    routing = expert_ids.reshape(-1)
    onehot = (routing[:, None] == jnp.arange(E, dtype=jnp.int32)[None, :]).astype(jnp.int32)
    position = jnp.sum((jnp.cumsum(onehot, axis=0) - onehot) * onehot, axis=1)
    slot_of = (routing * CAP + position).reshape(token_count, 2)
    slot_index = jnp.arange(slot_total, dtype=jnp.int32)
    select_first = slot_of[:, 0:1] == slot_index[None, :]
    select_second = slot_of[:, 1:2] == slot_index[None, :]
    picker = jnp.logical_or(select_first, select_second)
    picker_bf = picker.astype(jnp.bfloat16)
    weighted = jnp.where(select_first, route_probs[:, 0:1], 0.0) + jnp.where(
        select_second, route_probs[:, 1:2], 0.0
    )
    contract_rows = (((0,), (0,)), ((), ()))
    back_dims = (((1,), (1,)), ((), ()))

    def place_rows(source, scaled):
        if scaled:
            placed = lax.dot_general(
                weighted,
                source.astype(jnp.float32),
                contract_rows,
                precision=lax.Precision.HIGHEST,
                preferred_element_type=jnp.float32,
            )
        else:
            placed = lax.dot_general(
                picker_bf, source, contract_rows, preferred_element_type=jnp.float32
            )
        placed = placed.astype(jnp.bfloat16).reshape(E, CAP, source.shape[1])
        return jnp.repeat(placed, groups, axis=0)

    def to_expert_layout(source, scaled):
        arrived = lax.all_to_all(
            place_rows(source, scaled), "dp", split_axis=0, concat_axis=0, tiled=True
        )
        mine = arrived.reshape(1, rows, feat)
        across = lax.all_to_all(
            jnp.broadcast_to(mine, (chips, rows, feat)), "fy", split_axis=0, concat_axis=0, tiled=True
        )
        both = lax.all_to_all(
            jnp.broadcast_to(across[:, None], (chips, cores, rows, feat)),
            "fc", split_axis=1, concat_axis=1, tiled=True,
        )
        return both.reshape(fsdp_count, rows, feat)

    def to_token_layout(partial_value):
        blocks = partial_value.astype(jnp.bfloat16).reshape(chips, cores, rows, feat)
        kept = lax.dynamic_index_in_dim(blocks, core, axis=1, keepdims=False)
        sent = lax.dynamic_index_in_dim(blocks, 1 - core, axis=1, keepdims=False)
        within = kept.astype(jnp.float32) + lax.ppermute(sent, "fc", swap).astype(jnp.float32)
        parts = lax.all_to_all(within.astype(jnp.bfloat16), "fy", split_axis=0, concat_axis=0, tiled=True)
        shares = jnp.sum(parts.astype(jnp.float32), axis=0).astype(jnp.bfloat16)
        returned = lax.all_to_all(
            shares.reshape(dp_count, CAP, feat),
            "dp",
            split_axis=0,
            concat_axis=0,
            tiled=True,
        ).astype(jnp.float32)
        return jnp.sum(returned.reshape(E, groups, CAP, feat), axis=1).reshape(slot_total, feat)

    gate_w3 = w_gate.reshape(fsdp_count, feat, hid)
    up_w3 = w_up.reshape(fsdp_count, feat, hid)
    down_w3 = w_down.reshape(hid, fsdp_count, feat)
    in_dims = (((0, 2), (0, 1)), ((), ()))

    expert_rows = to_expert_layout(tokens, False)
    gate_proj = lax.dot_general(expert_rows, gate_w3, in_dims, preferred_element_type=jnp.float32)
    up_proj = lax.dot_general(expert_rows, up_w3, in_dims, preferred_element_type=jnp.float32)
    sigmoid_gate = jax.nn.sigmoid(gate_proj)
    activated = gate_proj * sigmoid_gate
    hidden = (activated * up_proj).astype(jnp.bfloat16)
    out_partial = jnp.einsum(
        "rh,hfd->frd", hidden, down_w3, preferred_element_type=jnp.float32
    )
    out_slots = to_token_layout(out_partial)
    first_pair = jnp.dot(
        select_first.astype(jnp.float32),
        out_slots,
        precision=lax.Precision.HIGHEST,
        preferred_element_type=jnp.float32,
    )
    second_pair = jnp.dot(
        select_second.astype(jnp.float32),
        out_slots,
        precision=lax.Precision.HIGHEST,
        preferred_element_type=jnp.float32,
    )
    mixed = (route_probs[:, 0:1] * first_pair + route_probs[:, 1:2] * second_pair).astype(
        jnp.bfloat16
    )
    grad_local = out_grad.astype(jnp.float32)
    prob_terms = jnp.stack(
        [jnp.sum(first_pair * grad_local, axis=1), jnp.sum(second_pair * grad_local, axis=1)],
        axis=1,
    )
    prob_grad = jnp.sum(lax.all_gather(prob_terms, ("fy", "fc"), axis=0, tiled=False), axis=0)
    grad_rows = to_expert_layout(out_grad, True)
    hidden_grad = lax.dot_general(grad_rows, down_w3, (((0, 2), (1, 2)), ((), ())),
                                  preferred_element_type=jnp.float32)
    gate_grad = (
        hidden_grad * up_proj * sigmoid_gate * (1.0 + gate_proj * (1.0 - sigmoid_gate))
    ).astype(jnp.bfloat16)
    up_grad = (hidden_grad * activated).astype(jnp.bfloat16)
    gate_weight_grad = jnp.einsum(
        "frd,rh->fdh", expert_rows, gate_grad, preferred_element_type=jnp.float32
    ).astype(jnp.bfloat16).reshape(fsdp_count * feat, hid)
    up_weight_grad = jnp.einsum(
        "frd,rh->fdh", expert_rows, up_grad, preferred_element_type=jnp.float32
    ).astype(jnp.bfloat16).reshape(fsdp_count * feat, hid)
    down_weight_grad = jnp.einsum(
        "rh,frd->hfd", hidden, grad_rows, preferred_element_type=jnp.float32
    ).astype(jnp.bfloat16).reshape(hid, model)
    input_partial = jnp.einsum(
        "rh,fdh->frd", gate_grad, gate_w3, preferred_element_type=jnp.float32
    )
    input_partial = input_partial + jnp.einsum(
        "rh,fdh->frd", up_grad, up_w3, preferred_element_type=jnp.float32
    )
    input_slots = to_token_layout(input_partial)
    token_grad = jnp.dot(
        picker.astype(jnp.float32),
        input_slots,
        precision=lax.Precision.HIGHEST,
        preferred_element_type=jnp.float32,
    ).astype(jnp.bfloat16)
    return (mixed, token_grad, prob_grad, gate_weight_grad, up_weight_grad, down_weight_grad)


def solution(mesh):
    dp_size, fsdp_size = mesh.devices.shape
    cores = 2
    split = Mesh(mesh.devices.reshape(dp_size, fsdp_size // cores, cores), ("dp", "fy", "fc"))
    fs = ("fy", "fc")
    placed = (
        P("dp", fs),
        P("dp", None),
        P("dp", None),
        P(None, ("dp",) + fs),
        P(None, ("dp",) + fs),
        P(("dp",) + fs, None),
        P("dp", fs),
    )
    return jax.shard_map(
        local,
        mesh=split,
        in_specs=placed,
        out_specs=(
            P("dp", fs),
            P("dp", fs),
            P("dp", None),
            P(None, ("dp",) + fs),
            P(None, ("dp",) + fs),
            P(("dp",) + fs, None),
        ),
        check_vma=False,
    )
```

```python
import jax
import jax.numpy as jnp
from jax import lax
from jax.sharding import Mesh, PartitionSpec as P

E = 8
CAP = 40


def local(tokens, expert_ids, route_probs, w_gate, w_up, w_down, out_grad):
    dp_count = lax.axis_size("dp")
    chips = lax.axis_size("fy")
    cores = lax.axis_size("fc")
    fsdp_count = chips * cores
    groups = dp_count // E
    token_count = tokens.shape[0]
    feat = tokens.shape[1]
    model = w_down.shape[1]
    hid = w_gate.shape[1]
    slot_total = E * CAP
    rows = dp_count * CAP
    core = lax.axis_index("fc")
    swap = [(0, 1), (1, 0)]
    routing = expert_ids.reshape(-1)
    onehot = (routing[:, None] == jnp.arange(E, dtype=jnp.int32)[None, :]).astype(jnp.int32)
    position = jnp.sum((jnp.cumsum(onehot, axis=0) - onehot) * onehot, axis=1)
    slot_of = (routing * CAP + position).reshape(token_count, 2)
    slot_index = jnp.arange(slot_total, dtype=jnp.int32)
    select_first = slot_of[:, 0:1] == slot_index[None, :]
    select_second = slot_of[:, 1:2] == slot_index[None, :]
    picker = jnp.logical_or(select_first, select_second)
    picker_bf = picker.astype(jnp.bfloat16)
    weighted = jnp.where(select_first, route_probs[:, 0:1], 0.0) + jnp.where(
        select_second, route_probs[:, 1:2], 0.0
    )
    contract_rows = (((0,), (0,)), ((), ()))
    back_dims = (((1,), (1,)), ((), ()))

    def place_rows(source, scaled):
        if scaled:
            placed = lax.dot_general(
                weighted,
                source.astype(jnp.float32),
                contract_rows,
                precision=lax.Precision.HIGHEST,
                preferred_element_type=jnp.float32,
            )
        else:
            placed = lax.dot_general(
                picker_bf, source, contract_rows, preferred_element_type=jnp.float32
            )
        placed = placed.astype(jnp.bfloat16).reshape(E, CAP, source.shape[1])
        return jnp.repeat(placed, groups, axis=0)

    def to_expert_layout(source, scaled):
        arrived = lax.all_to_all(
            place_rows(source, scaled), "dp", split_axis=0, concat_axis=0, tiled=True
        )
        across = lax.all_gather(arrived.reshape(rows, feat), "fy", axis=0, tiled=False)
        return across

    def join_cores(across):
        both = lax.all_to_all(
            jnp.broadcast_to(across[:, None], (chips, cores, rows, feat)),
            "fc", split_axis=1, concat_axis=1, tiled=True,
        )
        return both.reshape(fsdp_count, rows, feat)

    def to_token_layout(partial_value):
        blocks = partial_value.astype(jnp.bfloat16).reshape(chips, cores, rows, feat)
        kept = lax.dynamic_index_in_dim(blocks, core, axis=1, keepdims=False)
        sent = lax.dynamic_index_in_dim(blocks, 1 - core, axis=1, keepdims=False)
        within = kept.astype(jnp.float32) + lax.ppermute(sent, "fc", swap).astype(jnp.float32)
        shares = lax.psum_scatter(within.astype(jnp.bfloat16), "fy", scatter_dimension=0, tiled=False)
        returned = lax.all_to_all(
            shares.reshape(dp_count, CAP, feat),
            "dp",
            split_axis=0,
            concat_axis=0,
            tiled=True,
        ).astype(jnp.float32)
        return jnp.sum(returned.reshape(E, groups, CAP, feat), axis=1).reshape(slot_total, feat)

    gate_w3 = w_gate.reshape(fsdp_count, feat, hid)
    up_w3 = w_up.reshape(fsdp_count, feat, hid)
    down_w3 = w_down.reshape(hid, fsdp_count, feat)
    in_dims = (((0, 2), (0, 1)), ((), ()))

    expert_rows = join_cores(to_expert_layout(tokens, False))
    gate_proj = lax.dot_general(expert_rows, gate_w3, in_dims, preferred_element_type=jnp.float32)
    up_proj = lax.dot_general(expert_rows, up_w3, in_dims, preferred_element_type=jnp.float32)
    sigmoid_gate = jax.nn.sigmoid(gate_proj)
    activated = gate_proj * sigmoid_gate
    hidden = (activated * up_proj).astype(jnp.bfloat16)
    out_partial = jnp.einsum(
        "rh,hfd->frd", hidden, down_w3, preferred_element_type=jnp.float32
    )
    grad_across = to_expert_layout(out_grad, True)
    out_partial, grad_across = lax.optimization_barrier((out_partial, grad_across))
    out_slots = to_token_layout(out_partial)
    first_pair = jnp.dot(
        select_first.astype(jnp.float32),
        out_slots,
        precision=lax.Precision.HIGHEST,
        preferred_element_type=jnp.float32,
    )
    second_pair = jnp.dot(
        select_second.astype(jnp.float32),
        out_slots,
        precision=lax.Precision.HIGHEST,
        preferred_element_type=jnp.float32,
    )
    mixed = (route_probs[:, 0:1] * first_pair + route_probs[:, 1:2] * second_pair).astype(
        jnp.bfloat16
    )
    grad_local = out_grad.astype(jnp.float32)
    prob_terms = jnp.stack(
        [jnp.sum(first_pair * grad_local, axis=1), jnp.sum(second_pair * grad_local, axis=1)],
        axis=1,
    )
    prob_grad = jnp.sum(lax.all_gather(prob_terms, ("fy", "fc"), axis=0, tiled=False), axis=0)
    grad_rows = join_cores(grad_across)
    hidden_grad = lax.dot_general(grad_rows, down_w3, (((0, 2), (1, 2)), ((), ())),
                                  preferred_element_type=jnp.float32)
    gate_grad = (
        hidden_grad * up_proj * sigmoid_gate * (1.0 + gate_proj * (1.0 - sigmoid_gate))
    ).astype(jnp.bfloat16)
    up_grad = (hidden_grad * activated).astype(jnp.bfloat16)
    gate_weight_grad = jnp.einsum(
        "frd,rh->fdh", expert_rows, gate_grad, preferred_element_type=jnp.float32
    ).astype(jnp.bfloat16).reshape(fsdp_count * feat, hid)
    up_weight_grad = jnp.einsum(
        "frd,rh->fdh", expert_rows, up_grad, preferred_element_type=jnp.float32
    ).astype(jnp.bfloat16).reshape(fsdp_count * feat, hid)
    down_weight_grad = jnp.einsum(
        "rh,frd->hfd", hidden, grad_rows, preferred_element_type=jnp.float32
    ).astype(jnp.bfloat16).reshape(hid, model)
    input_partial = jnp.einsum(
        "rh,fdh->frd", gate_grad, gate_w3, preferred_element_type=jnp.float32
    )
    input_partial = input_partial + jnp.einsum(
        "rh,fdh->frd", up_grad, up_w3, preferred_element_type=jnp.float32
    )
    input_slots = to_token_layout(input_partial)
    token_grad = jnp.dot(
        picker.astype(jnp.float32),
        input_slots,
        precision=lax.Precision.HIGHEST,
        preferred_element_type=jnp.float32,
    ).astype(jnp.bfloat16)
    return (mixed, token_grad, prob_grad, gate_weight_grad, up_weight_grad, down_weight_grad)


def solution(mesh):
    dp_size, fsdp_size = mesh.devices.shape
    cores = 2
    split = Mesh(mesh.devices.reshape(dp_size, fsdp_size // cores, cores), ("dp", "fy", "fc"))
    fs = ("fy", "fc")
    placed = (
        P("dp", fs),
        P("dp", None),
        P("dp", None),
        P(None, ("dp",) + fs),
        P(None, ("dp",) + fs),
        P(("dp",) + fs, None),
        P("dp", fs),
    )
    return jax.shard_map(
        local,
        mesh=split,
        in_specs=placed,
        out_specs=(
            P("dp", fs),
            P("dp", fs),
            P("dp", None),
            P(None, ("dp",) + fs),
            P(None, ("dp",) + fs),
            P(("dp",) + fs, None),
        ),
        check_vma=False,
    )
```

```python
import jax
import jax.numpy as jnp
from jax import lax
from jax.sharding import Mesh, PartitionSpec as P

E = 8
CAP = 40


def local(tokens, expert_ids, route_probs, w_gate, w_up, w_down, out_grad):
    dp_count = lax.axis_size("dp")
    chips = lax.axis_size("fy")
    cores = lax.axis_size("fc")
    fsdp_count = chips * cores
    groups = dp_count // E
    token_count = tokens.shape[0]
    feat = tokens.shape[1]
    model = w_down.shape[1]
    hid = w_gate.shape[1]
    slot_total = E * CAP
    rows = dp_count * CAP
    core = lax.axis_index("fc")
    swap = [(0, 1), (1, 0)]
    routing = expert_ids.reshape(-1)
    onehot = (routing[:, None] == jnp.arange(E, dtype=jnp.int32)[None, :]).astype(jnp.int32)
    position = jnp.sum((jnp.cumsum(onehot, axis=0) - onehot) * onehot, axis=1)
    slot_of = (routing * CAP + position).reshape(token_count, 2)
    slot_index = jnp.arange(slot_total, dtype=jnp.int32)
    select_first = slot_of[:, 0:1] == slot_index[None, :]
    select_second = slot_of[:, 1:2] == slot_index[None, :]
    picker = jnp.logical_or(select_first, select_second)
    picker_bf = picker.astype(jnp.bfloat16)
    weighted = jnp.where(select_first, route_probs[:, 0:1], 0.0) + jnp.where(
        select_second, route_probs[:, 1:2], 0.0
    )
    contract_rows = (((0,), (0,)), ((), ()))
    back_dims = (((1,), (1,)), ((), ()))

    def place_rows(source, scaled):
        if scaled:
            placed = lax.dot_general(
                weighted,
                source.astype(jnp.float32),
                contract_rows,
                precision=lax.Precision.HIGHEST,
                preferred_element_type=jnp.float32,
            )
        else:
            placed = lax.dot_general(
                picker_bf, source, contract_rows, preferred_element_type=jnp.float32
            )
        placed = placed.astype(jnp.bfloat16).reshape(E, CAP, source.shape[1])
        return jnp.repeat(placed, groups, axis=0)

    def to_expert_layout(source, scaled):
        arrived = lax.all_to_all(
            place_rows(source, scaled), "dp", split_axis=0, concat_axis=0, tiled=True
        )
        across = lax.all_gather(arrived.reshape(rows, feat), "fy", axis=0, tiled=False)
        return across

    def join_cores(across):
        both = lax.all_to_all(
            jnp.broadcast_to(across[:, None], (chips, cores, rows, feat)),
            "fc", split_axis=1, concat_axis=1, tiled=True,
        )
        return both.reshape(fsdp_count, rows, feat)

    def swap_cores(partial_value):
        blocks = partial_value.astype(jnp.bfloat16).reshape(chips, cores, rows, feat)
        kept = lax.dynamic_index_in_dim(blocks, core, axis=1, keepdims=False)
        sent = lax.dynamic_index_in_dim(blocks, 1 - core, axis=1, keepdims=False)
        within = kept.astype(jnp.float32) + lax.ppermute(sent, "fc", swap).astype(jnp.float32)
        return within.astype(jnp.bfloat16)

    def scatter_chips(within):
        return lax.psum_scatter(within, "fy", scatter_dimension=0, tiled=False)

    def to_token_layout(shares):
        returned = lax.all_to_all(
            shares.reshape(dp_count, CAP, feat),
            "dp",
            split_axis=0,
            concat_axis=0,
            tiled=True,
        ).astype(jnp.float32)
        return jnp.sum(returned.reshape(E, groups, CAP, feat), axis=1).reshape(slot_total, feat)

    gate_w3 = w_gate.reshape(fsdp_count, feat, hid)
    up_w3 = w_up.reshape(fsdp_count, feat, hid)
    down_w3 = w_down.reshape(hid, fsdp_count, feat)
    in_dims = (((0, 2), (0, 1)), ((), ()))

    expert_rows = join_cores(to_expert_layout(tokens, False))
    gate_proj = lax.dot_general(expert_rows, gate_w3, in_dims, preferred_element_type=jnp.float32)
    up_proj = lax.dot_general(expert_rows, up_w3, in_dims, preferred_element_type=jnp.float32)
    sigmoid_gate = jax.nn.sigmoid(gate_proj)
    activated = gate_proj * sigmoid_gate
    hidden = (activated * up_proj).astype(jnp.bfloat16)
    out_partial = jnp.einsum(
        "rh,hfd->frd", hidden, down_w3, preferred_element_type=jnp.float32
    )
    grad_across = to_expert_layout(out_grad, True)
    out_within, grad_across = lax.optimization_barrier((swap_cores(out_partial), grad_across))
    out_slots = to_token_layout(scatter_chips(out_within))
    first_pair = jnp.dot(
        select_first.astype(jnp.float32),
        out_slots,
        precision=lax.Precision.HIGHEST,
        preferred_element_type=jnp.float32,
    )
    second_pair = jnp.dot(
        select_second.astype(jnp.float32),
        out_slots,
        precision=lax.Precision.HIGHEST,
        preferred_element_type=jnp.float32,
    )
    mixed = (route_probs[:, 0:1] * first_pair + route_probs[:, 1:2] * second_pair).astype(
        jnp.bfloat16
    )
    grad_local = out_grad.astype(jnp.float32)
    prob_terms = jnp.stack(
        [jnp.sum(first_pair * grad_local, axis=1), jnp.sum(second_pair * grad_local, axis=1)],
        axis=1,
    )
    prob_grad = jnp.sum(lax.all_gather(prob_terms, ("fy", "fc"), axis=0, tiled=False), axis=0)
    grad_rows = join_cores(grad_across)
    hidden_grad = lax.dot_general(grad_rows, down_w3, (((0, 2), (1, 2)), ((), ())),
                                  preferred_element_type=jnp.float32)
    gate_grad = (
        hidden_grad * up_proj * sigmoid_gate * (1.0 + gate_proj * (1.0 - sigmoid_gate))
    ).astype(jnp.bfloat16)
    up_grad = (hidden_grad * activated).astype(jnp.bfloat16)
    gate_weight_grad = jnp.einsum(
        "frd,rh->fdh", expert_rows, gate_grad, preferred_element_type=jnp.float32
    ).astype(jnp.bfloat16).reshape(fsdp_count * feat, hid)
    up_weight_grad = jnp.einsum(
        "frd,rh->fdh", expert_rows, up_grad, preferred_element_type=jnp.float32
    ).astype(jnp.bfloat16).reshape(fsdp_count * feat, hid)
    down_weight_grad = jnp.einsum(
        "rh,frd->hfd", hidden, grad_rows, preferred_element_type=jnp.float32
    ).astype(jnp.bfloat16).reshape(hid, model)
    input_partial = jnp.einsum(
        "rh,fdh->frd", gate_grad, gate_w3, preferred_element_type=jnp.float32
    )
    input_partial = input_partial + jnp.einsum(
        "rh,fdh->frd", up_grad, up_w3, preferred_element_type=jnp.float32
    )
    input_shares = scatter_chips(swap_cores(input_partial))
    prob_grad, input_shares = lax.optimization_barrier((prob_grad, input_shares))
    input_slots = to_token_layout(input_shares)
    token_grad = jnp.dot(
        picker.astype(jnp.float32),
        input_slots,
        precision=lax.Precision.HIGHEST,
        preferred_element_type=jnp.float32,
    ).astype(jnp.bfloat16)
    return (mixed, token_grad, prob_grad, gate_weight_grad, up_weight_grad, down_weight_grad)


def solution(mesh):
    dp_size, fsdp_size = mesh.devices.shape
    cores = 2
    split = Mesh(mesh.devices.reshape(dp_size, fsdp_size // cores, cores), ("dp", "fy", "fc"))
    fs = ("fy", "fc")
    placed = (
        P("dp", fs),
        P("dp", None),
        P("dp", None),
        P(None, ("dp",) + fs),
        P(None, ("dp",) + fs),
        P(("dp",) + fs, None),
        P("dp", fs),
    )
    return jax.shard_map(
        local,
        mesh=split,
        in_specs=placed,
        out_specs=(
            P("dp", fs),
            P("dp", fs),
            P("dp", None),
            P(None, ("dp",) + fs),
            P(None, ("dp",) + fs),
            P(("dp",) + fs, None),
        ),
        check_vma=False,
    )
```

```python
import jax
import jax.numpy as jnp
from jax import lax
from jax.sharding import Mesh, PartitionSpec as P

E = 8
CAP = 40


def local(tokens, expert_ids, route_probs, w_gate, w_up, w_down, out_grad):
    dp_count = lax.axis_size("dp")
    chips = lax.axis_size("fy")
    cores = lax.axis_size("fc")
    fsdp_count = chips * cores
    groups = dp_count // E
    token_count = tokens.shape[0]
    feat = tokens.shape[1]
    model = w_down.shape[1]
    hid = w_gate.shape[1]
    slot_total = E * CAP
    rows = dp_count * CAP
    split_rows = rows // 2
    core = lax.axis_index("fc")
    swap = [(0, 1), (1, 0)]
    routing = expert_ids.reshape(-1)
    onehot = (routing[:, None] == jnp.arange(E, dtype=jnp.int32)[None, :]).astype(jnp.int32)
    position = jnp.sum((jnp.cumsum(onehot, axis=0) - onehot) * onehot, axis=1)
    slot_of = (routing * CAP + position).reshape(token_count, 2)
    slot_index = jnp.arange(slot_total, dtype=jnp.int32)
    select_first = slot_of[:, 0:1] == slot_index[None, :]
    select_second = slot_of[:, 1:2] == slot_index[None, :]
    picker = jnp.logical_or(select_first, select_second)
    picker_bf = picker.astype(jnp.bfloat16)
    weighted = jnp.where(select_first, route_probs[:, 0:1], 0.0) + jnp.where(
        select_second, route_probs[:, 1:2], 0.0
    )
    contract_rows = (((0,), (0,)), ((), ()))
    back_dims = (((1,), (1,)), ((), ()))

    def place_rows(source, scaled):
        if scaled:
            placed = lax.dot_general(
                weighted,
                source.astype(jnp.float32),
                contract_rows,
                precision=lax.Precision.HIGHEST,
                preferred_element_type=jnp.float32,
            )
        else:
            placed = lax.dot_general(
                picker_bf, source, contract_rows, preferred_element_type=jnp.float32
            )
        placed = placed.astype(jnp.bfloat16).reshape(E, CAP, source.shape[1])
        return jnp.repeat(placed, groups, axis=0)

    def to_expert_layout(source, scaled):
        arrived = lax.all_to_all(
            place_rows(source, scaled), "dp", split_axis=0, concat_axis=0, tiled=True
        )
        flat = arrived.reshape(rows, feat)
        first = lax.all_gather(flat[:split_rows], "fy", axis=0, tiled=False)
        copies = jnp.broadcast_to(flat[None, split_rows:], (chips, rows - split_rows, feat))
        second = lax.all_to_all(copies, "fy", split_axis=0, concat_axis=0, tiled=True)
        return jnp.concatenate([first, second], axis=1)

    def join_cores(across):
        both = lax.all_to_all(
            jnp.broadcast_to(across[:, None], (chips, cores, rows, feat)),
            "fc", split_axis=1, concat_axis=1, tiled=True,
        )
        return both.reshape(fsdp_count, rows, feat)

    def swap_cores(partial_value):
        blocks = partial_value.astype(jnp.bfloat16).reshape(chips, cores, rows, feat)
        kept = lax.dynamic_index_in_dim(blocks, core, axis=1, keepdims=False)
        sent = lax.dynamic_index_in_dim(blocks, 1 - core, axis=1, keepdims=False)
        within = kept.astype(jnp.float32) + lax.ppermute(sent, "fc", swap).astype(jnp.float32)
        return within.astype(jnp.bfloat16)

    def scatter_chips(within):
        first = lax.psum_scatter(within[:, :split_rows], "fy", scatter_dimension=0, tiled=False)
        parts = lax.all_to_all(within[:, split_rows:], "fy", split_axis=0, concat_axis=0, tiled=True)
        second = jnp.sum(parts.astype(jnp.float32), axis=0).astype(jnp.bfloat16)
        return jnp.concatenate([first, second], axis=0)

    def to_token_layout(shares):
        returned = lax.all_to_all(
            shares.reshape(dp_count, CAP, feat),
            "dp",
            split_axis=0,
            concat_axis=0,
            tiled=True,
        ).astype(jnp.float32)
        return jnp.sum(returned.reshape(E, groups, CAP, feat), axis=1).reshape(slot_total, feat)

    gate_w3 = w_gate.reshape(fsdp_count, feat, hid)
    up_w3 = w_up.reshape(fsdp_count, feat, hid)
    down_w3 = w_down.reshape(hid, fsdp_count, feat)
    in_dims = (((0, 2), (0, 1)), ((), ()))

    expert_rows = join_cores(to_expert_layout(tokens, False))
    gate_proj = lax.dot_general(expert_rows, gate_w3, in_dims, preferred_element_type=jnp.float32)
    up_proj = lax.dot_general(expert_rows, up_w3, in_dims, preferred_element_type=jnp.float32)
    sigmoid_gate = jax.nn.sigmoid(gate_proj)
    activated = gate_proj * sigmoid_gate
    hidden = (activated * up_proj).astype(jnp.bfloat16)
    out_partial = jnp.einsum(
        "rh,hfd->frd", hidden, down_w3, preferred_element_type=jnp.float32
    )
    grad_across = to_expert_layout(out_grad, True)
    out_within, grad_across = lax.optimization_barrier((swap_cores(out_partial), grad_across))
    out_slots = to_token_layout(scatter_chips(out_within))
    first_pair = jnp.dot(
        select_first.astype(jnp.float32),
        out_slots,
        precision=lax.Precision.HIGHEST,
        preferred_element_type=jnp.float32,
    )
    second_pair = jnp.dot(
        select_second.astype(jnp.float32),
        out_slots,
        precision=lax.Precision.HIGHEST,
        preferred_element_type=jnp.float32,
    )
    mixed = (route_probs[:, 0:1] * first_pair + route_probs[:, 1:2] * second_pair).astype(
        jnp.bfloat16
    )
    grad_local = out_grad.astype(jnp.float32)
    prob_terms = jnp.stack(
        [jnp.sum(first_pair * grad_local, axis=1), jnp.sum(second_pair * grad_local, axis=1)],
        axis=1,
    )
    prob_grad = jnp.sum(lax.all_gather(prob_terms, ("fy", "fc"), axis=0, tiled=False), axis=0)
    grad_rows = join_cores(grad_across)
    hidden_grad = lax.dot_general(grad_rows, down_w3, (((0, 2), (1, 2)), ((), ())),
                                  preferred_element_type=jnp.float32)
    gate_grad = (
        hidden_grad * up_proj * sigmoid_gate * (1.0 + gate_proj * (1.0 - sigmoid_gate))
    ).astype(jnp.bfloat16)
    up_grad = (hidden_grad * activated).astype(jnp.bfloat16)
    gate_weight_grad = jnp.einsum(
        "frd,rh->fdh", expert_rows, gate_grad, preferred_element_type=jnp.float32
    ).astype(jnp.bfloat16).reshape(fsdp_count * feat, hid)
    up_weight_grad = jnp.einsum(
        "frd,rh->fdh", expert_rows, up_grad, preferred_element_type=jnp.float32
    ).astype(jnp.bfloat16).reshape(fsdp_count * feat, hid)
    down_weight_grad = jnp.einsum(
        "rh,frd->hfd", hidden, grad_rows, preferred_element_type=jnp.float32
    ).astype(jnp.bfloat16).reshape(hid, model)
    input_partial = jnp.einsum(
        "rh,fdh->frd", gate_grad, gate_w3, preferred_element_type=jnp.float32
    )
    input_partial = input_partial + jnp.einsum(
        "rh,fdh->frd", up_grad, up_w3, preferred_element_type=jnp.float32
    )
    input_shares = scatter_chips(swap_cores(input_partial))
    prob_grad, input_shares = lax.optimization_barrier((prob_grad, input_shares))
    input_slots = to_token_layout(input_shares)
    token_grad = jnp.dot(
        picker.astype(jnp.float32),
        input_slots,
        precision=lax.Precision.HIGHEST,
        preferred_element_type=jnp.float32,
    ).astype(jnp.bfloat16)
    return (mixed, token_grad, prob_grad, gate_weight_grad, up_weight_grad, down_weight_grad)


def solution(mesh):
    dp_size, fsdp_size = mesh.devices.shape
    cores = 2
    split = Mesh(mesh.devices.reshape(dp_size, fsdp_size // cores, cores), ("dp", "fy", "fc"))
    fs = ("fy", "fc")
    placed = (
        P("dp", fs),
        P("dp", None),
        P("dp", None),
        P(None, ("dp",) + fs),
        P(None, ("dp",) + fs),
        P(("dp",) + fs, None),
        P("dp", fs),
    )
    return jax.shard_map(
        local,
        mesh=split,
        in_specs=placed,
        out_specs=(
            P("dp", fs),
            P("dp", fs),
            P("dp", None),
            P(None, ("dp",) + fs),
            P(None, ("dp",) + fs),
            P(("dp",) + fs, None),
        ),
        check_vma=False,
    )
```

```python
import jax
import jax.numpy as jnp
from jax import lax
from jax.sharding import Mesh, PartitionSpec as P

E = 8
CAP = 40


def local(tokens, expert_ids, route_probs, w_gate, w_up, w_down, out_grad):
    dp_count = lax.axis_size("dp")
    chips = lax.axis_size("fy")
    cores = lax.axis_size("fc")
    fsdp_count = chips * cores
    groups = dp_count // E
    token_count = tokens.shape[0]
    feat = tokens.shape[1]
    model = w_down.shape[1]
    hid = w_gate.shape[1]
    slot_total = E * CAP
    rows = dp_count * CAP
    split_rows = rows // 2
    chip = lax.axis_index("fy")
    ring_up = [(i, (i + 1) % chips) for i in range(chips)]
    ring_down = [(i, (i - 1) % chips) for i in range(chips)]
    core = lax.axis_index("fc")
    swap = [(0, 1), (1, 0)]
    routing = expert_ids.reshape(-1)
    onehot = (routing[:, None] == jnp.arange(E, dtype=jnp.int32)[None, :]).astype(jnp.int32)
    position = jnp.sum((jnp.cumsum(onehot, axis=0) - onehot) * onehot, axis=1)
    slot_of = (routing * CAP + position).reshape(token_count, 2)
    slot_index = jnp.arange(slot_total, dtype=jnp.int32)
    select_first = slot_of[:, 0:1] == slot_index[None, :]
    select_second = slot_of[:, 1:2] == slot_index[None, :]
    picker = jnp.logical_or(select_first, select_second)
    picker_bf = picker.astype(jnp.bfloat16)
    weighted = jnp.where(select_first, route_probs[:, 0:1], 0.0) + jnp.where(
        select_second, route_probs[:, 1:2], 0.0
    )
    contract_rows = (((0,), (0,)), ((), ()))
    back_dims = (((1,), (1,)), ((), ()))

    def place_rows(source, scaled):
        if scaled:
            placed = lax.dot_general(
                weighted,
                source.astype(jnp.float32),
                contract_rows,
                precision=lax.Precision.HIGHEST,
                preferred_element_type=jnp.float32,
            )
        else:
            placed = lax.dot_general(
                picker_bf, source, contract_rows, preferred_element_type=jnp.float32
            )
        placed = placed.astype(jnp.bfloat16).reshape(E, CAP, source.shape[1])
        return jnp.repeat(placed, groups, axis=0)

    def to_expert_layout(source, scaled):
        arrived = lax.all_to_all(
            place_rows(source, scaled), "dp", split_axis=0, concat_axis=0, tiled=True
        )
        mine = arrived.reshape(rows, feat)
        from_below = lax.ppermute(mine, "fy", ring_up)
        from_above = lax.ppermute(mine, "fy", ring_down)
        far = jnp.concatenate([lax.ppermute(from_below[:split_rows], "fy", ring_up),
                               lax.ppermute(from_above[split_rows:], "fy", ring_down)], axis=0)
        relative = jnp.stack([mine, from_below, far, from_above])
        return jnp.take(relative, (chip - jnp.arange(chips)) % chips, axis=0)

    def join_cores(across):
        both = lax.all_to_all(
            jnp.broadcast_to(across[:, None], (chips, cores, rows, feat)),
            "fc", split_axis=1, concat_axis=1, tiled=True,
        )
        return both.reshape(fsdp_count, rows, feat)

    def swap_cores(partial_value):
        blocks = partial_value.astype(jnp.bfloat16).reshape(chips, cores, rows, feat)
        kept = lax.dynamic_index_in_dim(blocks, core, axis=1, keepdims=False)
        sent = lax.dynamic_index_in_dim(blocks, 1 - core, axis=1, keepdims=False)
        within = kept.astype(jnp.float32) + lax.ppermute(sent, "fc", swap).astype(jnp.float32)
        return within.astype(jnp.bfloat16)

    def scatter_chips(within):
        def block(offset):
            return lax.dynamic_index_in_dim(within, (chip + offset) % chips, axis=0, keepdims=False)

        far = block(2)
        got_up = lax.ppermute(far[:split_rows], "fy", ring_up).astype(jnp.float32)
        got_down = lax.ppermute(far[split_rows:], "fy", ring_down).astype(jnp.float32)
        up_next = block(1).astype(jnp.float32)
        up_next = jnp.concatenate([up_next[:split_rows] + got_up, up_next[split_rows:]], axis=0)
        down_next = block(-1).astype(jnp.float32)
        down_next = jnp.concatenate([down_next[:split_rows], down_next[split_rows:] + got_down], axis=0)
        from_below = lax.ppermute(up_next.astype(jnp.bfloat16), "fy", ring_up).astype(jnp.float32)
        from_above = lax.ppermute(down_next.astype(jnp.bfloat16), "fy", ring_down).astype(jnp.float32)
        return (block(0).astype(jnp.float32) + from_below + from_above).astype(jnp.bfloat16)

    def to_token_layout(shares):
        returned = lax.all_to_all(
            shares.reshape(dp_count, CAP, feat),
            "dp",
            split_axis=0,
            concat_axis=0,
            tiled=True,
        ).astype(jnp.float32)
        return jnp.sum(returned.reshape(E, groups, CAP, feat), axis=1).reshape(slot_total, feat)

    gate_w3 = w_gate.reshape(fsdp_count, feat, hid)
    up_w3 = w_up.reshape(fsdp_count, feat, hid)
    down_w3 = w_down.reshape(hid, fsdp_count, feat)
    in_dims = (((0, 2), (0, 1)), ((), ()))

    expert_rows = join_cores(to_expert_layout(tokens, False))
    gate_proj = lax.dot_general(expert_rows, gate_w3, in_dims, preferred_element_type=jnp.float32)
    up_proj = lax.dot_general(expert_rows, up_w3, in_dims, preferred_element_type=jnp.float32)
    sigmoid_gate = jax.nn.sigmoid(gate_proj)
    activated = gate_proj * sigmoid_gate
    hidden = (activated * up_proj).astype(jnp.bfloat16)
    out_partial = jnp.einsum(
        "rh,hfd->frd", hidden, down_w3, preferred_element_type=jnp.float32
    )
    grad_across = to_expert_layout(out_grad, True)
    out_within, grad_across = lax.optimization_barrier((swap_cores(out_partial), grad_across))
    out_slots = to_token_layout(scatter_chips(out_within))
    first_pair = jnp.dot(
        select_first.astype(jnp.float32),
        out_slots,
        precision=lax.Precision.HIGHEST,
        preferred_element_type=jnp.float32,
    )
    second_pair = jnp.dot(
        select_second.astype(jnp.float32),
        out_slots,
        precision=lax.Precision.HIGHEST,
        preferred_element_type=jnp.float32,
    )
    mixed = (route_probs[:, 0:1] * first_pair + route_probs[:, 1:2] * second_pair).astype(
        jnp.bfloat16
    )
    grad_local = out_grad.astype(jnp.float32)
    prob_terms = jnp.stack(
        [jnp.sum(first_pair * grad_local, axis=1), jnp.sum(second_pair * grad_local, axis=1)],
        axis=1,
    )
    prob_grad = jnp.sum(lax.all_gather(prob_terms, ("fy", "fc"), axis=0, tiled=False), axis=0)
    grad_rows = join_cores(grad_across)
    hidden_grad = lax.dot_general(grad_rows, down_w3, (((0, 2), (1, 2)), ((), ())),
                                  preferred_element_type=jnp.float32)
    gate_grad = (
        hidden_grad * up_proj * sigmoid_gate * (1.0 + gate_proj * (1.0 - sigmoid_gate))
    ).astype(jnp.bfloat16)
    up_grad = (hidden_grad * activated).astype(jnp.bfloat16)
    gate_weight_grad = jnp.einsum(
        "frd,rh->fdh", expert_rows, gate_grad, preferred_element_type=jnp.float32
    ).astype(jnp.bfloat16).reshape(fsdp_count * feat, hid)
    up_weight_grad = jnp.einsum(
        "frd,rh->fdh", expert_rows, up_grad, preferred_element_type=jnp.float32
    ).astype(jnp.bfloat16).reshape(fsdp_count * feat, hid)
    down_weight_grad = jnp.einsum(
        "rh,frd->hfd", hidden, grad_rows, preferred_element_type=jnp.float32
    ).astype(jnp.bfloat16).reshape(hid, model)
    input_partial = jnp.einsum(
        "rh,fdh->frd", gate_grad, gate_w3, preferred_element_type=jnp.float32
    )
    input_partial = input_partial + jnp.einsum(
        "rh,fdh->frd", up_grad, up_w3, preferred_element_type=jnp.float32
    )
    input_shares = scatter_chips(swap_cores(input_partial))
    prob_grad, input_shares = lax.optimization_barrier((prob_grad, input_shares))
    input_slots = to_token_layout(input_shares)
    token_grad = jnp.dot(
        picker.astype(jnp.float32),
        input_slots,
        precision=lax.Precision.HIGHEST,
        preferred_element_type=jnp.float32,
    ).astype(jnp.bfloat16)
    return (mixed, token_grad, prob_grad, gate_weight_grad, up_weight_grad, down_weight_grad)


def solution(mesh):
    dp_size, fsdp_size = mesh.devices.shape
    cores = 2
    split = Mesh(mesh.devices.reshape(dp_size, fsdp_size // cores, cores), ("dp", "fy", "fc"))
    fs = ("fy", "fc")
    placed = (
        P("dp", fs),
        P("dp", None),
        P("dp", None),
        P(None, ("dp",) + fs),
        P(None, ("dp",) + fs),
        P(("dp",) + fs, None),
        P("dp", fs),
    )
    return jax.shard_map(
        local,
        mesh=split,
        in_specs=placed,
        out_specs=(
            P("dp", fs),
            P("dp", fs),
            P("dp", None),
            P(None, ("dp",) + fs),
            P(None, ("dp",) + fs),
            P(("dp",) + fs, None),
        ),
        check_vma=False,
    )
```

```python
import jax
import jax.numpy as jnp
from jax import lax
from jax.sharding import Mesh, PartitionSpec as P

E = 8
CAP = 40


def local(tokens, expert_ids, route_probs, w_gate, w_up, w_down, out_grad):
    dp_count = lax.axis_size("dp")
    chips = lax.axis_size("fy")
    cores = lax.axis_size("fc")
    fsdp_count = chips * cores
    groups = dp_count // E
    token_count = tokens.shape[0]
    feat = tokens.shape[1]
    model = w_down.shape[1]
    hid = w_gate.shape[1]
    slot_total = E * CAP
    rows = dp_count * CAP
    core = lax.axis_index("fc")
    swap = [(0, 1), (1, 0)]
    routing = expert_ids.reshape(-1)
    onehot = (routing[:, None] == jnp.arange(E, dtype=jnp.int32)[None, :]).astype(jnp.int32)
    position = jnp.sum((jnp.cumsum(onehot, axis=0) - onehot) * onehot, axis=1)
    slot_of = (routing * CAP + position).reshape(token_count, 2)
    slot_index = jnp.arange(slot_total, dtype=jnp.int32)
    select_first = slot_of[:, 0:1] == slot_index[None, :]
    select_second = slot_of[:, 1:2] == slot_index[None, :]
    picker = jnp.logical_or(select_first, select_second)
    picker_bf = picker.astype(jnp.bfloat16)
    weighted = jnp.where(select_first, route_probs[:, 0:1], 0.0) + jnp.where(
        select_second, route_probs[:, 1:2], 0.0
    )
    contract_rows = (((0,), (0,)), ((), ()))
    back_dims = (((1,), (1,)), ((), ()))

    def place_rows(source, scaled):
        if scaled:
            placed = lax.dot_general(
                weighted,
                source.astype(jnp.float32),
                contract_rows,
                precision=lax.Precision.HIGHEST,
                preferred_element_type=jnp.float32,
            )
        else:
            placed = lax.dot_general(
                picker_bf, source, contract_rows, preferred_element_type=jnp.float32
            )
        placed = placed.astype(jnp.bfloat16).reshape(E, CAP, source.shape[1])
        return jnp.repeat(placed, groups, axis=0)

    def to_expert_layout(source, scaled):
        arrived = lax.all_to_all(
            place_rows(source, scaled), "dp", split_axis=0, concat_axis=0, tiled=True
        )
        across = lax.all_gather(arrived.reshape(rows, feat), "fy", axis=0, tiled=False)
        return across

    def join_cores(across):
        both = lax.all_to_all(
            jnp.broadcast_to(across[:, None], (chips, cores, rows, feat)),
            "fc", split_axis=1, concat_axis=1, tiled=True,
        )
        return both.reshape(fsdp_count, rows, feat)

    def swap_cores(partial_value):
        blocks = partial_value.astype(jnp.bfloat16).reshape(chips, cores, rows, feat)
        kept = lax.dynamic_index_in_dim(blocks, core, axis=1, keepdims=False)
        sent = lax.dynamic_index_in_dim(blocks, 1 - core, axis=1, keepdims=False)
        within = kept.astype(jnp.float32) + lax.ppermute(sent, "fc", swap).astype(jnp.float32)
        return within.astype(jnp.bfloat16)

    def scatter_chips(within):
        return lax.psum_scatter(within, "fy", scatter_dimension=0, tiled=False)

    def to_token_layout(shares):
        returned = lax.all_to_all(
            shares.reshape(dp_count, CAP, feat),
            "dp",
            split_axis=0,
            concat_axis=0,
            tiled=True,
        ).astype(jnp.float32)
        return jnp.sum(returned.reshape(E, groups, CAP, feat), axis=1).reshape(slot_total, feat)

    gate_w3 = w_gate.reshape(fsdp_count, feat, hid)
    up_w3 = w_up.reshape(fsdp_count, feat, hid)
    down_w3 = w_down.reshape(hid, fsdp_count, feat)
    in_dims = (((0, 2), (0, 1)), ((), ()))

    expert_rows = join_cores(to_expert_layout(tokens, False))
    gate_proj = lax.dot_general(expert_rows, gate_w3, in_dims, preferred_element_type=jnp.float32)
    up_proj = lax.dot_general(expert_rows, up_w3, in_dims, preferred_element_type=jnp.float32)
    sigmoid_gate = jax.nn.sigmoid(gate_proj)
    activated = gate_proj * sigmoid_gate
    hidden = (activated * up_proj).astype(jnp.bfloat16)
    out_partial = jnp.einsum(
        "rh,hfd->frd", hidden, down_w3, preferred_element_type=jnp.float32
    )
    grad_across = to_expert_layout(out_grad, True)
    out_within, grad_across = lax.optimization_barrier((swap_cores(out_partial), grad_across))
    out_slots = to_token_layout(scatter_chips(out_within))
    first_pair = jnp.dot(
        select_first.astype(jnp.float32),
        out_slots,
        precision=lax.Precision.HIGHEST,
        preferred_element_type=jnp.float32,
    )
    second_pair = jnp.dot(
        select_second.astype(jnp.float32),
        out_slots,
        precision=lax.Precision.HIGHEST,
        preferred_element_type=jnp.float32,
    )
    mixed = (route_probs[:, 0:1] * first_pair + route_probs[:, 1:2] * second_pair).astype(
        jnp.bfloat16
    )
    grad_local = out_grad.astype(jnp.float32)
    prob_terms = jnp.stack(
        [jnp.sum(first_pair * grad_local, axis=1), jnp.sum(second_pair * grad_local, axis=1)],
        axis=1,
    )
    prob_grad = jnp.sum(lax.all_gather(prob_terms, ("fy", "fc"), axis=0, tiled=False), axis=0)
    grad_rows = join_cores(grad_across)
    hidden_grad = lax.dot_general(grad_rows, down_w3, (((0, 2), (1, 2)), ((), ())),
                                  preferred_element_type=jnp.float32)
    gate_grad = (
        hidden_grad * up_proj * sigmoid_gate * (1.0 + gate_proj * (1.0 - sigmoid_gate))
    ).astype(jnp.bfloat16)
    up_grad = (hidden_grad * activated).astype(jnp.bfloat16)
    gate_weight_grad = jnp.einsum(
        "frd,rh->fdh", expert_rows, gate_grad, preferred_element_type=jnp.float32
    ).astype(jnp.bfloat16).reshape(fsdp_count * feat, hid)
    up_weight_grad = jnp.einsum(
        "frd,rh->fdh", expert_rows, up_grad, preferred_element_type=jnp.float32
    ).astype(jnp.bfloat16).reshape(fsdp_count * feat, hid)
    down_weight_grad = jnp.einsum(
        "hr,frd->hfd", hidden.T, grad_rows, preferred_element_type=jnp.float32
    ).astype(jnp.bfloat16).reshape(hid, model)
    input_partial = jnp.einsum(
        "rh,fdh->frd", gate_grad, gate_w3, preferred_element_type=jnp.float32
    )
    input_partial = input_partial + jnp.einsum(
        "rh,fdh->frd", up_grad, up_w3, preferred_element_type=jnp.float32
    )
    input_shares = scatter_chips(swap_cores(input_partial))
    prob_grad, gate_weight_grad, up_weight_grad, down_weight_grad, input_shares = lax.optimization_barrier(
        (prob_grad, gate_weight_grad, up_weight_grad, down_weight_grad, input_shares))
    input_slots = to_token_layout(input_shares)
    token_grad = jnp.dot(
        picker.astype(jnp.float32),
        input_slots,
        precision=lax.Precision.HIGHEST,
        preferred_element_type=jnp.float32,
    ).astype(jnp.bfloat16)
    return (mixed, token_grad, prob_grad, gate_weight_grad, up_weight_grad, down_weight_grad)


def solution(mesh):
    dp_size, fsdp_size = mesh.devices.shape
    cores = 2
    split = Mesh(mesh.devices.reshape(dp_size, fsdp_size // cores, cores), ("dp", "fy", "fc"))
    fs = ("fy", "fc")
    placed = (
        P("dp", fs),
        P("dp", None),
        P("dp", None),
        P(None, ("dp",) + fs),
        P(None, ("dp",) + fs),
        P(("dp",) + fs, None),
        P("dp", fs),
    )
    return jax.shard_map(
        local,
        mesh=split,
        in_specs=placed,
        out_specs=(
            P("dp", fs),
            P("dp", fs),
            P("dp", None),
            P(None, ("dp",) + fs),
            P(None, ("dp",) + fs),
            P(("dp",) + fs, None),
        ),
        check_vma=False,
    )
```

```python
import jax
import jax.numpy as jnp
from jax import lax
from jax.sharding import Mesh, PartitionSpec as P

E = 8
CAP = 40


def local(tokens, expert_ids, route_probs, w_gate, w_up, w_down, out_grad):
    dp_count = lax.axis_size("dp")
    chips = lax.axis_size("fy")
    cores = lax.axis_size("fc")
    fsdp_count = chips * cores
    groups = dp_count // E
    token_count = tokens.shape[0]
    feat = tokens.shape[1]
    model = w_down.shape[1]
    hid = w_gate.shape[1]
    slot_total = E * CAP
    rows = dp_count * CAP
    core = lax.axis_index("fc")
    swap = [(0, 1), (1, 0)]
    routing = expert_ids.reshape(-1)
    onehot = (routing[:, None] == jnp.arange(E, dtype=jnp.int32)[None, :]).astype(jnp.int32)
    position = jnp.sum((jnp.cumsum(onehot, axis=0) - onehot) * onehot, axis=1)
    slot_of = (routing * CAP + position).reshape(token_count, 2)
    slot_index = jnp.arange(slot_total, dtype=jnp.int32)
    select_first = slot_of[:, 0:1] == slot_index[None, :]
    select_second = slot_of[:, 1:2] == slot_index[None, :]
    picker = jnp.logical_or(select_first, select_second)
    picker_bf = picker.astype(jnp.bfloat16)
    weighted = jnp.where(select_first, route_probs[:, 0:1], 0.0) + jnp.where(
        select_second, route_probs[:, 1:2], 0.0
    )
    contract_rows = (((0,), (0,)), ((), ()))
    back_dims = (((1,), (1,)), ((), ()))

    def place_rows(source, scaled):
        if scaled:
            placed = lax.dot_general(
                weighted,
                source.astype(jnp.float32),
                contract_rows,
                precision=lax.Precision.HIGHEST,
                preferred_element_type=jnp.float32,
            )
        else:
            placed = lax.dot_general(
                picker_bf, source, contract_rows, preferred_element_type=jnp.float32
            )
        placed = placed.astype(jnp.bfloat16).reshape(E, CAP, source.shape[1])
        return jnp.repeat(placed, groups, axis=0)

    def to_expert_layout(source, scaled):
        arrived = lax.all_to_all(
            place_rows(source, scaled), "dp", split_axis=0, concat_axis=0, tiled=True
        )
        across = lax.all_gather(arrived.reshape(rows, feat), "fy", axis=0, tiled=False)
        return across

    def join_cores(across):
        by_row = jnp.transpose(across, (1, 0, 2))[:, :, None, :]
        both = lax.all_to_all(
            jnp.broadcast_to(by_row, (rows, chips, cores, feat)),
            "fc", split_axis=2, concat_axis=2, tiled=True,
        )
        return both.reshape(rows, fsdp_count * feat)

    def swap_cores(partial_value):
        blocks = partial_value.astype(jnp.bfloat16).reshape(chips, cores, rows, feat)
        kept = lax.dynamic_index_in_dim(blocks, core, axis=1, keepdims=False)
        sent = lax.dynamic_index_in_dim(blocks, 1 - core, axis=1, keepdims=False)
        within = kept.astype(jnp.float32) + lax.ppermute(sent, "fc", swap).astype(jnp.float32)
        return within.astype(jnp.bfloat16)

    def scatter_chips(within):
        return lax.psum_scatter(within, "fy", scatter_dimension=0, tiled=False)

    def to_token_layout(shares):
        returned = lax.all_to_all(
            shares.reshape(dp_count, CAP, feat),
            "dp",
            split_axis=0,
            concat_axis=0,
            tiled=True,
        ).astype(jnp.float32)
        return jnp.sum(returned.reshape(E, groups, CAP, feat), axis=1).reshape(slot_total, feat)

    gate_w3 = w_gate.reshape(fsdp_count, feat, hid)
    up_w3 = w_up.reshape(fsdp_count, feat, hid)
    down_w3 = w_down.reshape(hid, fsdp_count, feat)


    expert_rows = join_cores(to_expert_layout(tokens, False))
    gate_proj = jnp.dot(expert_rows, w_gate, preferred_element_type=jnp.float32)
    up_proj = jnp.dot(expert_rows, w_up, preferred_element_type=jnp.float32)
    sigmoid_gate = jax.nn.sigmoid(gate_proj)
    activated = gate_proj * sigmoid_gate
    hidden = (activated * up_proj).astype(jnp.bfloat16)
    out_partial = jnp.einsum(
        "rh,hfd->frd", hidden, down_w3, preferred_element_type=jnp.float32
    )
    grad_across = to_expert_layout(out_grad, True)
    out_within, grad_across = lax.optimization_barrier((swap_cores(out_partial), grad_across))
    out_slots = to_token_layout(scatter_chips(out_within))
    first_pair = jnp.dot(
        select_first.astype(jnp.float32),
        out_slots,
        precision=lax.Precision.HIGHEST,
        preferred_element_type=jnp.float32,
    )
    second_pair = jnp.dot(
        select_second.astype(jnp.float32),
        out_slots,
        precision=lax.Precision.HIGHEST,
        preferred_element_type=jnp.float32,
    )
    mixed = (route_probs[:, 0:1] * first_pair + route_probs[:, 1:2] * second_pair).astype(
        jnp.bfloat16
    )
    grad_local = out_grad.astype(jnp.float32)
    prob_terms = jnp.stack(
        [jnp.sum(first_pair * grad_local, axis=1), jnp.sum(second_pair * grad_local, axis=1)],
        axis=1,
    )
    prob_grad = jnp.sum(lax.all_gather(prob_terms, ("fy", "fc"), axis=0, tiled=False), axis=0)
    grad_rows = join_cores(grad_across)
    hidden_grad = lax.dot_general(grad_rows, w_down, back_dims, preferred_element_type=jnp.float32)
    gate_grad = (
        hidden_grad * up_proj * sigmoid_gate * (1.0 + gate_proj * (1.0 - sigmoid_gate))
    ).astype(jnp.bfloat16)
    up_grad = (hidden_grad * activated).astype(jnp.bfloat16)
    out_slots, expert_rows, gate_grad_w, up_grad_w, grad_rows_w = lax.optimization_barrier(
        (out_slots, expert_rows, gate_grad, up_grad, grad_rows))
    gate_weight_grad = lax.dot_general(
        expert_rows, gate_grad_w, contract_rows, preferred_element_type=jnp.float32
    ).astype(jnp.bfloat16)
    up_weight_grad = lax.dot_general(
        expert_rows, up_grad_w, contract_rows, preferred_element_type=jnp.float32
    ).astype(jnp.bfloat16)
    down_weight_grad = lax.dot_general(
        hidden, grad_rows_w, contract_rows, preferred_element_type=jnp.float32
    ).astype(jnp.bfloat16)
    input_partial = jnp.einsum(
        "rh,fdh->frd", gate_grad, gate_w3, preferred_element_type=jnp.float32
    )
    input_partial = input_partial + jnp.einsum(
        "rh,fdh->frd", up_grad, up_w3, preferred_element_type=jnp.float32
    )
    input_shares = scatter_chips(swap_cores(input_partial))
    prob_grad, gate_weight_grad, up_weight_grad, down_weight_grad, input_shares = lax.optimization_barrier(
        (prob_grad, gate_weight_grad, up_weight_grad, down_weight_grad, input_shares))
    input_slots = to_token_layout(input_shares)
    token_grad = jnp.dot(
        picker.astype(jnp.float32),
        input_slots,
        precision=lax.Precision.HIGHEST,
        preferred_element_type=jnp.float32,
    ).astype(jnp.bfloat16)
    return (mixed, token_grad, prob_grad, gate_weight_grad, up_weight_grad, down_weight_grad)


def solution(mesh):
    dp_size, fsdp_size = mesh.devices.shape
    cores = 2
    split = Mesh(mesh.devices.reshape(dp_size, fsdp_size // cores, cores), ("dp", "fy", "fc"))
    fs = ("fy", "fc")
    placed = (
        P("dp", fs),
        P("dp", None),
        P("dp", None),
        P(None, ("dp",) + fs),
        P(None, ("dp",) + fs),
        P(("dp",) + fs, None),
        P("dp", fs),
    )
    return jax.shard_map(
        local,
        mesh=split,
        in_specs=placed,
        out_specs=(
            P("dp", fs),
            P("dp", fs),
            P("dp", None),
            P(None, ("dp",) + fs),
            P(None, ("dp",) + fs),
            P(("dp",) + fs, None),
        ),
        check_vma=False,
    )
```

```python
import jax
import jax.numpy as jnp
from jax import lax
from jax.sharding import Mesh, PartitionSpec as P

E = 8
CAP = 40


def local(tokens, expert_ids, route_probs, w_gate, w_up, w_down, out_grad):
    dp_count = lax.axis_size("dp")
    chips = lax.axis_size("fy")
    cores = lax.axis_size("fc")
    fsdp_count = chips * cores
    groups = dp_count // E
    token_count = tokens.shape[0]
    feat = tokens.shape[1]
    model = w_down.shape[1]
    hid = w_gate.shape[1]
    slot_total = E * CAP
    rows = dp_count * CAP
    core = lax.axis_index("fc")
    swap = [(0, 1), (1, 0)]
    routing = expert_ids.reshape(-1)
    onehot = (routing[:, None] == jnp.arange(E, dtype=jnp.int32)[None, :]).astype(jnp.int32)
    position = jnp.sum((jnp.cumsum(onehot, axis=0) - onehot) * onehot, axis=1)
    slot_of = (routing * CAP + position).reshape(token_count, 2)
    slot_index = jnp.arange(slot_total, dtype=jnp.int32)
    select_first = slot_of[:, 0:1] == slot_index[None, :]
    select_second = slot_of[:, 1:2] == slot_index[None, :]
    picker = jnp.logical_or(select_first, select_second)
    picker_bf = picker.astype(jnp.bfloat16)
    weighted = jnp.where(select_first, route_probs[:, 0:1], 0.0) + jnp.where(
        select_second, route_probs[:, 1:2], 0.0
    )
    contract_rows = (((0,), (0,)), ((), ()))
    back_dims = (((1,), (1,)), ((), ()))

    def place_rows(source, scaled):
        if scaled:
            placed = lax.dot_general(
                weighted,
                source.astype(jnp.float32),
                contract_rows,
                precision=lax.Precision.HIGHEST,
                preferred_element_type=jnp.float32,
            )
        else:
            placed = lax.dot_general(
                picker_bf, source, contract_rows, preferred_element_type=jnp.float32
            )
        placed = placed.astype(jnp.bfloat16).reshape(E, CAP, source.shape[1])
        return jnp.repeat(placed, groups, axis=0)

    def to_expert_layout(source, scaled):
        arrived = lax.all_to_all(
            place_rows(source, scaled), "dp", split_axis=0, concat_axis=0, tiled=True
        )
        across = lax.all_gather(arrived.reshape(rows, feat), "fy", axis=0, tiled=False)
        return across

    def join_cores(across):
        both = lax.all_to_all(
            jnp.broadcast_to(across[:, None], (chips, cores, rows, feat)),
            "fc", split_axis=1, concat_axis=1, tiled=True,
        )
        return both.reshape(fsdp_count, rows, feat)

    def swap_cores(partial_value):
        blocks = partial_value.astype(jnp.bfloat16).reshape(chips, cores, rows, feat)
        kept = lax.dynamic_index_in_dim(blocks, core, axis=1, keepdims=False)
        sent = lax.dynamic_index_in_dim(blocks, 1 - core, axis=1, keepdims=False)
        within = kept.astype(jnp.float32) + lax.ppermute(sent, "fc", swap).astype(jnp.float32)
        return within.astype(jnp.bfloat16)

    def scatter_chips(within):
        return lax.psum_scatter(within, "fy", scatter_dimension=0, tiled=False)

    def to_token_layout(shares):
        returned = lax.all_to_all(
            shares.reshape(dp_count, CAP, feat),
            "dp",
            split_axis=0,
            concat_axis=0,
            tiled=True,
        ).astype(jnp.float32)
        return jnp.sum(returned.reshape(E, groups, CAP, feat), axis=1).reshape(slot_total, feat)

    gate_w3 = w_gate.reshape(fsdp_count, feat, hid)
    up_w3 = w_up.reshape(fsdp_count, feat, hid)
    down_w3 = w_down.reshape(hid, fsdp_count, feat)
    in_dims = (((0, 2), (0, 1)), ((), ()))

    expert_rows = join_cores(to_expert_layout(tokens, False))
    gate_proj = lax.dot_general(expert_rows, gate_w3, in_dims, preferred_element_type=jnp.float32)
    up_proj = lax.dot_general(expert_rows, up_w3, in_dims, preferred_element_type=jnp.float32)
    sigmoid_gate = jax.nn.sigmoid(gate_proj)
    activated = gate_proj * sigmoid_gate
    hidden = (activated * up_proj).astype(jnp.bfloat16)
    out_partial = jnp.einsum(
        "rh,hfd->frd", hidden, down_w3, preferred_element_type=jnp.float32
    )
    grad_across = to_expert_layout(out_grad, True)
    out_within, grad_across = lax.optimization_barrier((swap_cores(out_partial), grad_across))
    out_slots = to_token_layout(scatter_chips(out_within))
    first_pair = jnp.dot(
        select_first.astype(jnp.float32),
        out_slots,
        precision=lax.Precision.HIGHEST,
        preferred_element_type=jnp.float32,
    )
    second_pair = jnp.dot(
        select_second.astype(jnp.float32),
        out_slots,
        precision=lax.Precision.HIGHEST,
        preferred_element_type=jnp.float32,
    )
    mixed = (route_probs[:, 0:1] * first_pair + route_probs[:, 1:2] * second_pair).astype(
        jnp.bfloat16
    )
    grad_local = out_grad.astype(jnp.float32)
    prob_terms = jnp.stack(
        [jnp.sum(first_pair * grad_local, axis=1), jnp.sum(second_pair * grad_local, axis=1)],
        axis=1,
    )
    padded = jnp.zeros((token_count, 128), jnp.float32).at[:, :2].set(prob_terms)
    prob_grad = lax.psum(padded, ("fy", "fc"))[:, :2]
    grad_rows = join_cores(grad_across)
    hidden_grad = lax.dot_general(grad_rows, down_w3, (((0, 2), (1, 2)), ((), ())),
                                  preferred_element_type=jnp.float32)
    gate_grad = (
        hidden_grad * up_proj * sigmoid_gate * (1.0 + gate_proj * (1.0 - sigmoid_gate))
    ).astype(jnp.bfloat16)
    up_grad = (hidden_grad * activated).astype(jnp.bfloat16)
    gate_weight_grad = jnp.einsum(
        "frd,rh->fdh", expert_rows, gate_grad, preferred_element_type=jnp.float32
    ).astype(jnp.bfloat16).reshape(fsdp_count * feat, hid)
    up_weight_grad = jnp.einsum(
        "frd,rh->fdh", expert_rows, up_grad, preferred_element_type=jnp.float32
    ).astype(jnp.bfloat16).reshape(fsdp_count * feat, hid)
    down_weight_grad = jnp.einsum(
        "hr,frd->hfd", hidden.T, grad_rows, preferred_element_type=jnp.float32
    ).astype(jnp.bfloat16).reshape(hid, model)
    input_partial = jnp.einsum(
        "rh,fdh->frd", gate_grad, gate_w3, preferred_element_type=jnp.float32
    )
    input_partial = input_partial + jnp.einsum(
        "rh,fdh->frd", up_grad, up_w3, preferred_element_type=jnp.float32
    )
    input_shares = scatter_chips(swap_cores(input_partial))
    prob_grad, gate_weight_grad, up_weight_grad, down_weight_grad, input_shares = lax.optimization_barrier(
        (prob_grad, gate_weight_grad, up_weight_grad, down_weight_grad, input_shares))
    input_slots = to_token_layout(input_shares)
    token_grad = jnp.dot(
        picker.astype(jnp.float32),
        input_slots,
        precision=lax.Precision.HIGHEST,
        preferred_element_type=jnp.float32,
    ).astype(jnp.bfloat16)
    return (mixed, token_grad, prob_grad, gate_weight_grad, up_weight_grad, down_weight_grad)


def solution(mesh):
    dp_size, fsdp_size = mesh.devices.shape
    cores = 2
    split = Mesh(mesh.devices.reshape(dp_size, fsdp_size // cores, cores), ("dp", "fy", "fc"))
    fs = ("fy", "fc")
    placed = (
        P("dp", fs),
        P("dp", None),
        P("dp", None),
        P(None, ("dp",) + fs),
        P(None, ("dp",) + fs),
        P(("dp",) + fs, None),
        P("dp", fs),
    )
    return jax.shard_map(
        local,
        mesh=split,
        in_specs=placed,
        out_specs=(
            P("dp", fs),
            P("dp", fs),
            P("dp", None),
            P(None, ("dp",) + fs),
            P(None, ("dp",) + fs),
            P(("dp",) + fs, None),
        ),
        check_vma=False,
    )
```

```python
import jax
import jax.numpy as jnp
from jax import lax
from jax.sharding import Mesh, PartitionSpec as P

E = 8
CAP = 40


def local(tokens, expert_ids, route_probs, w_gate, w_up, w_down, out_grad):
    dp_count = lax.axis_size("dp")
    chips = lax.axis_size("fy")
    cores = lax.axis_size("fc")
    fsdp_count = chips * cores
    groups = dp_count // E
    token_count = tokens.shape[0]
    feat = tokens.shape[1]
    model = w_down.shape[1]
    hid = w_gate.shape[1]
    slot_total = E * CAP
    rows = dp_count * CAP
    core = lax.axis_index("fc")
    swap = [(0, 1), (1, 0)]
    routing = expert_ids.reshape(-1)
    onehot = (routing[:, None] == jnp.arange(E, dtype=jnp.int32)[None, :]).astype(jnp.int32)
    position = jnp.sum((jnp.cumsum(onehot, axis=0) - onehot) * onehot, axis=1)
    slot_of = (routing * CAP + position).reshape(token_count, 2)
    slot_index = jnp.arange(slot_total, dtype=jnp.int32)
    select_first = slot_of[:, 0:1] == slot_index[None, :]
    select_second = slot_of[:, 1:2] == slot_index[None, :]
    picker = jnp.logical_or(select_first, select_second)
    picker_bf = picker.astype(jnp.bfloat16)
    weighted = jnp.where(select_first, route_probs[:, 0:1], 0.0) + jnp.where(
        select_second, route_probs[:, 1:2], 0.0
    )
    contract_rows = (((0,), (0,)), ((), ()))
    back_dims = (((1,), (1,)), ((), ()))

    def place_rows(source, scaled):
        if scaled:
            placed = lax.dot_general(
                weighted,
                source.astype(jnp.float32),
                contract_rows,
                precision=lax.Precision.HIGHEST,
                preferred_element_type=jnp.float32,
            )
        else:
            placed = lax.dot_general(
                picker_bf, source, contract_rows, preferred_element_type=jnp.float32
            )
        placed = placed.astype(jnp.bfloat16).reshape(E, CAP, source.shape[1])
        return jnp.repeat(placed, groups, axis=0)

    def to_expert_layout(source, scaled):
        arrived = lax.all_to_all(
            place_rows(source, scaled), "dp", split_axis=0, concat_axis=0, tiled=True
        )
        across = lax.all_gather(arrived.reshape(rows, feat), "fy", axis=0, tiled=False)
        return across

    def join_cores(across):
        both = lax.all_to_all(
            jnp.broadcast_to(across[:, None], (chips, cores, rows, feat)),
            "fc", split_axis=1, concat_axis=1, tiled=True,
        )
        return both.reshape(fsdp_count, rows, feat)

    def swap_cores(partial_value):
        blocks = partial_value.astype(jnp.bfloat16).reshape(chips, cores, rows, feat)
        kept = lax.dynamic_index_in_dim(blocks, core, axis=1, keepdims=False)
        sent = lax.dynamic_index_in_dim(blocks, 1 - core, axis=1, keepdims=False)
        within = kept.astype(jnp.float32) + lax.ppermute(sent, "fc", swap).astype(jnp.float32)
        return within.astype(jnp.bfloat16)

    def scatter_chips(within):
        return lax.psum_scatter(within, "fy", scatter_dimension=0, tiled=False)

    def to_token_layout(shares):
        returned = lax.all_to_all(
            shares.reshape(dp_count, CAP, feat),
            "dp",
            split_axis=0,
            concat_axis=0,
            tiled=True,
        ).astype(jnp.float32)
        return jnp.sum(returned.reshape(E, groups, CAP, feat), axis=1).reshape(slot_total, feat)

    gate_w3 = w_gate.reshape(fsdp_count, feat, hid)
    up_w3 = w_up.reshape(fsdp_count, feat, hid)
    down_w3 = w_down.reshape(hid, fsdp_count, feat)
    in_dims = (((0, 2), (0, 1)), ((), ()))

    expert_rows = join_cores(to_expert_layout(tokens, False))
    gate_proj = lax.dot_general(expert_rows, gate_w3, in_dims, preferred_element_type=jnp.float32)
    up_proj = lax.dot_general(expert_rows, up_w3, in_dims, preferred_element_type=jnp.float32)
    sigmoid_gate = jax.nn.sigmoid(gate_proj)
    activated = gate_proj * sigmoid_gate
    hidden = (activated * up_proj).astype(jnp.bfloat16)
    out_partial = jnp.einsum(
        "rh,hfd->frd", hidden, down_w3, preferred_element_type=jnp.float32
    )
    grad_across = to_expert_layout(out_grad, True)
    out_within, grad_across = lax.optimization_barrier((swap_cores(out_partial), grad_across))
    out_slots = to_token_layout(scatter_chips(out_within))
    first_pair = jnp.dot(
        select_first.astype(jnp.float32),
        out_slots,
        precision=lax.Precision.HIGHEST,
        preferred_element_type=jnp.float32,
    )
    second_pair = jnp.dot(
        select_second.astype(jnp.float32),
        out_slots,
        precision=lax.Precision.HIGHEST,
        preferred_element_type=jnp.float32,
    )
    mixed = (route_probs[:, 0:1] * first_pair + route_probs[:, 1:2] * second_pair).astype(
        jnp.bfloat16
    )
    grad_local = out_grad.astype(jnp.float32)
    prob_terms = jnp.stack(
        [jnp.sum(first_pair * grad_local, axis=1), jnp.sum(second_pair * grad_local, axis=1)],
        axis=1,
    )
    prob_grad = jnp.sum(lax.all_gather(prob_terms, ("fy", "fc"), axis=0, tiled=False), axis=0)
    grad_rows = join_cores(grad_across)
    hidden_grad = lax.dot_general(grad_rows, down_w3, (((0, 2), (1, 2)), ((), ())),
                                  preferred_element_type=jnp.float32)
    gate_grad = (
        hidden_grad * up_proj * sigmoid_gate * (1.0 + gate_proj * (1.0 - sigmoid_gate))
    ).astype(jnp.bfloat16)
    up_grad = (hidden_grad * activated).astype(jnp.bfloat16)
    out_slots, rows_w, gate_grad_w, up_grad_w, grad_rows_w, hidden_w = lax.optimization_barrier(
        (out_slots, expert_rows, gate_grad, up_grad, grad_rows, hidden))
    gate_weight_grad = jnp.einsum(
        "frd,rh->fdh", rows_w, gate_grad_w, preferred_element_type=jnp.float32
    ).astype(jnp.bfloat16).reshape(fsdp_count * feat, hid)
    up_weight_grad = jnp.einsum(
        "frd,rh->fdh", rows_w, up_grad_w, preferred_element_type=jnp.float32
    ).astype(jnp.bfloat16).reshape(fsdp_count * feat, hid)
    down_weight_grad = jnp.einsum(
        "rh,frd->hfd", hidden_w, grad_rows_w, preferred_element_type=jnp.float32
    ).astype(jnp.bfloat16).reshape(hid, model)
    input_partial = jnp.einsum(
        "rh,fdh->frd", gate_grad, gate_w3, preferred_element_type=jnp.float32
    )
    input_partial = input_partial + jnp.einsum(
        "rh,fdh->frd", up_grad, up_w3, preferred_element_type=jnp.float32
    )
    input_shares = scatter_chips(swap_cores(input_partial))
    prob_grad, gate_weight_grad, up_weight_grad, down_weight_grad, input_shares = lax.optimization_barrier(
        (prob_grad, gate_weight_grad, up_weight_grad, down_weight_grad, input_shares))
    input_slots = to_token_layout(input_shares)
    token_grad = jnp.dot(
        picker.astype(jnp.float32),
        input_slots,
        precision=lax.Precision.HIGHEST,
        preferred_element_type=jnp.float32,
    ).astype(jnp.bfloat16)
    return (mixed, token_grad, prob_grad, gate_weight_grad, up_weight_grad, down_weight_grad)


def solution(mesh):
    dp_size, fsdp_size = mesh.devices.shape
    cores = 2
    split = Mesh(mesh.devices.reshape(dp_size, fsdp_size // cores, cores), ("dp", "fy", "fc"))
    fs = ("fy", "fc")
    placed = (
        P("dp", fs),
        P("dp", None),
        P("dp", None),
        P(None, ("dp",) + fs),
        P(None, ("dp",) + fs),
        P(("dp",) + fs, None),
        P("dp", fs),
    )
    return jax.shard_map(
        local,
        mesh=split,
        in_specs=placed,
        out_specs=(
            P("dp", fs),
            P("dp", fs),
            P("dp", None),
            P(None, ("dp",) + fs),
            P(None, ("dp",) + fs),
            P(("dp",) + fs, None),
        ),
        check_vma=False,
    )
```

```python
import jax
import jax.numpy as jnp
from jax import lax
from jax.sharding import Mesh, PartitionSpec as P

E = 8
CAP = 40


def local(tokens, expert_ids, route_probs, w_gate, w_up, w_down, out_grad):
    dp_count = lax.axis_size("dp")
    chips = lax.axis_size("fy")
    cores = lax.axis_size("fc")
    fsdp_count = chips * cores
    groups = dp_count // E
    token_count = tokens.shape[0]
    feat = tokens.shape[1]
    model = w_down.shape[1]
    hid = w_gate.shape[1]
    slot_total = E * CAP
    rows = dp_count * CAP
    core = lax.axis_index("fc")
    swap = [(0, 1), (1, 0)]
    routing = expert_ids.reshape(-1)
    onehot = (routing[:, None] == jnp.arange(E, dtype=jnp.int32)[None, :]).astype(jnp.int32)
    position = jnp.sum((jnp.cumsum(onehot, axis=0) - onehot) * onehot, axis=1)
    slot_of = (routing * CAP + position).reshape(token_count, 2)
    slot_index = jnp.arange(slot_total, dtype=jnp.int32)
    select_first = slot_of[:, 0:1] == slot_index[None, :]
    select_second = slot_of[:, 1:2] == slot_index[None, :]
    picker = jnp.logical_or(select_first, select_second)
    picker_bf = picker.astype(jnp.bfloat16)
    weighted = jnp.where(select_first, route_probs[:, 0:1], 0.0) + jnp.where(
        select_second, route_probs[:, 1:2], 0.0
    )
    contract_rows = (((0,), (0,)), ((), ()))
    back_dims = (((1,), (1,)), ((), ()))

    def place_rows(source, scaled):
        if scaled:
            placed = lax.dot_general(
                weighted,
                source.astype(jnp.float32),
                contract_rows,
                precision=lax.Precision.HIGHEST,
                preferred_element_type=jnp.float32,
            )
        else:
            placed = lax.dot_general(
                picker_bf, source, contract_rows, preferred_element_type=jnp.float32
            )
        placed = placed.astype(jnp.bfloat16).reshape(E, CAP, source.shape[1])
        return jnp.repeat(placed, groups, axis=0)

    def to_expert_layout(source, scaled):
        arrived = lax.all_to_all(
            place_rows(source, scaled), "dp", split_axis=0, concat_axis=0, tiled=True
        )
        across = lax.all_gather(arrived.reshape(rows, feat), "fy", axis=0, tiled=False)
        return across

    def join_cores(across):
        both = lax.all_to_all(
            jnp.broadcast_to(across[:, None], (chips, cores, rows, feat)),
            "fc", split_axis=1, concat_axis=1, tiled=True,
        )
        return both.reshape(fsdp_count, rows, feat)

    def swap_cores(partial_value):
        blocks = partial_value.astype(jnp.bfloat16).reshape(chips, cores, rows, feat)
        kept = lax.dynamic_index_in_dim(blocks, core, axis=1, keepdims=False)
        sent = lax.dynamic_index_in_dim(blocks, 1 - core, axis=1, keepdims=False)
        within = kept.astype(jnp.float32) + lax.ppermute(sent, "fc", swap).astype(jnp.float32)
        return within.astype(jnp.bfloat16)

    def scatter_chips(within):
        return lax.psum_scatter(within, "fy", scatter_dimension=0, tiled=False)

    def to_token_layout(shares):
        returned = lax.all_to_all(
            shares.reshape(dp_count, CAP, feat),
            "dp",
            split_axis=0,
            concat_axis=0,
            tiled=True,
        ).astype(jnp.float32)
        return jnp.sum(returned.reshape(E, groups, CAP, feat), axis=1).reshape(slot_total, feat)

    gate_w3 = w_gate.reshape(fsdp_count, feat, hid)
    up_w3 = w_up.reshape(fsdp_count, feat, hid)
    down_w3 = w_down.reshape(hid, fsdp_count, feat)
    in_dims = (((0, 2), (0, 1)), ((), ()))

    expert_rows = join_cores(to_expert_layout(tokens, False))
    gate_proj = lax.dot_general(expert_rows, gate_w3, in_dims, preferred_element_type=jnp.float32)
    up_proj = lax.dot_general(expert_rows, up_w3, in_dims, preferred_element_type=jnp.float32)
    sigmoid_gate = jax.nn.sigmoid(gate_proj)
    activated = gate_proj * sigmoid_gate
    hidden = (activated * up_proj).astype(jnp.bfloat16)
    out_partial = jnp.einsum(
        "rh,hfd->frd", hidden, down_w3, preferred_element_type=jnp.float32
    )
    grad_across = to_expert_layout(out_grad, True)
    out_within, grad_across = lax.optimization_barrier((swap_cores(out_partial), grad_across))
    out_slots = to_token_layout(scatter_chips(out_within))
    first_pair = jnp.dot(
        select_first.astype(jnp.float32),
        out_slots,
        precision=lax.Precision.HIGHEST,
        preferred_element_type=jnp.float32,
    )
    second_pair = jnp.dot(
        select_second.astype(jnp.float32),
        out_slots,
        precision=lax.Precision.HIGHEST,
        preferred_element_type=jnp.float32,
    )
    mixed = (route_probs[:, 0:1] * first_pair + route_probs[:, 1:2] * second_pair).astype(
        jnp.bfloat16
    )
    grad_local = out_grad.astype(jnp.float32)
    prob_terms = jnp.stack(
        [jnp.sum(first_pair * grad_local, axis=1), jnp.sum(second_pair * grad_local, axis=1)],
        axis=1,
    )
    prob_grad = jnp.sum(lax.all_gather(prob_terms, ("fy", "fc"), axis=0, tiled=False), axis=0)
    grad_rows = join_cores(grad_across)
    hidden_grad = lax.dot_general(grad_rows, down_w3, (((0, 2), (1, 2)), ((), ())),
                                  preferred_element_type=jnp.float32)
    gate_grad = (
        hidden_grad * up_proj * sigmoid_gate * (1.0 + gate_proj * (1.0 - sigmoid_gate))
    ).astype(jnp.bfloat16)
    up_grad = (hidden_grad * activated).astype(jnp.bfloat16)
    gate_weight_grad = jnp.einsum(
        "frd,rh->fdh", expert_rows, gate_grad, preferred_element_type=jnp.float32
    ).astype(jnp.bfloat16).reshape(fsdp_count * feat, hid)
    down_weight_grad = jnp.einsum(
        "hr,frd->hfd", hidden.T, grad_rows, preferred_element_type=jnp.float32
    ).astype(jnp.bfloat16).reshape(hid, model)
    input_partial = jnp.einsum(
        "rh,fdh->frd", gate_grad, gate_w3, preferred_element_type=jnp.float32
    )
    input_partial = input_partial + jnp.einsum(
        "rh,fdh->frd", up_grad, up_w3, preferred_element_type=jnp.float32
    )
    input_shares = scatter_chips(swap_cores(input_partial))
    prob_grad, gate_weight_grad, down_weight_grad, input_shares, up_grad_late = lax.optimization_barrier(
        (prob_grad, gate_weight_grad, down_weight_grad, input_shares, up_grad))
    up_weight_grad = jnp.einsum(
        "frd,rh->fdh", expert_rows, up_grad_late, preferred_element_type=jnp.float32
    ).astype(jnp.bfloat16).reshape(fsdp_count * feat, hid)
    input_slots = to_token_layout(input_shares)
    token_grad = jnp.dot(
        picker.astype(jnp.float32),
        input_slots,
        precision=lax.Precision.HIGHEST,
        preferred_element_type=jnp.float32,
    ).astype(jnp.bfloat16)
    return (mixed, token_grad, prob_grad, gate_weight_grad, up_weight_grad, down_weight_grad)


def solution(mesh):
    dp_size, fsdp_size = mesh.devices.shape
    cores = 2
    split = Mesh(mesh.devices.reshape(dp_size, fsdp_size // cores, cores), ("dp", "fy", "fc"))
    fs = ("fy", "fc")
    placed = (
        P("dp", fs),
        P("dp", None),
        P("dp", None),
        P(None, ("dp",) + fs),
        P(None, ("dp",) + fs),
        P(("dp",) + fs, None),
        P("dp", fs),
    )
    return jax.shard_map(
        local,
        mesh=split,
        in_specs=placed,
        out_specs=(
            P("dp", fs),
            P("dp", fs),
            P("dp", None),
            P(None, ("dp",) + fs),
            P(None, ("dp",) + fs),
            P(("dp",) + fs, None),
        ),
        check_vma=False,
    )
```

```python
import jax
import jax.numpy as jnp
from jax import lax
from jax.sharding import Mesh, PartitionSpec as P

E = 8
CAP = 40


def local(tokens, expert_ids, route_probs, w_gate, w_up, w_down, out_grad):
    dp_count = lax.axis_size("dp")
    chips = lax.axis_size("fy")
    cores = lax.axis_size("fc")
    fsdp_count = chips * cores
    groups = dp_count // E
    token_count = tokens.shape[0]
    feat = tokens.shape[1]
    model = w_down.shape[1]
    hid = w_gate.shape[1]
    slot_total = E * CAP
    rows = dp_count * CAP
    core = lax.axis_index("fc")
    swap = [(0, 1), (1, 0)]
    routing = expert_ids.reshape(-1)
    onehot = (routing[:, None] == jnp.arange(E, dtype=jnp.int32)[None, :]).astype(jnp.int32)
    position = jnp.sum((jnp.cumsum(onehot, axis=0) - onehot) * onehot, axis=1)
    slot_of = (routing * CAP + position).reshape(token_count, 2)
    slot_index = jnp.arange(slot_total, dtype=jnp.int32)
    select_first = slot_of[:, 0:1] == slot_index[None, :]
    select_second = slot_of[:, 1:2] == slot_index[None, :]
    picker = jnp.logical_or(select_first, select_second)
    picker_bf = picker.astype(jnp.bfloat16)
    weighted = jnp.where(select_first, route_probs[:, 0:1], 0.0) + jnp.where(
        select_second, route_probs[:, 1:2], 0.0
    )
    contract_rows = (((0,), (0,)), ((), ()))
    back_dims = (((1,), (1,)), ((), ()))

    def place_rows(source, scaled):
        if scaled:
            placed = lax.dot_general(
                weighted,
                source.astype(jnp.float32),
                contract_rows,
                precision=lax.Precision.HIGHEST,
                preferred_element_type=jnp.float32,
            )
        else:
            placed = lax.dot_general(
                picker_bf, source, contract_rows, preferred_element_type=jnp.float32
            )
        placed = placed.astype(jnp.bfloat16).reshape(E, CAP, source.shape[1])
        return jnp.repeat(placed, groups, axis=0)

    def to_expert_layout(source, scaled):
        arrived = lax.all_to_all(
            place_rows(source, scaled), "dp", split_axis=0, concat_axis=0, tiled=True
        )
        across = lax.all_gather(arrived.reshape(rows, feat), "fy", axis=0, tiled=False)
        return across

    def join_cores(across):
        both = lax.all_to_all(
            jnp.broadcast_to(across[:, None], (chips, cores, rows, feat)),
            "fc", split_axis=1, concat_axis=1, tiled=True,
        )
        return both.reshape(fsdp_count, rows, feat)

    def swap_cores(partial_value):
        blocks = partial_value.astype(jnp.bfloat16).reshape(chips, cores, rows, feat)
        kept = lax.dynamic_index_in_dim(blocks, core, axis=1, keepdims=False)
        sent = lax.dynamic_index_in_dim(blocks, 1 - core, axis=1, keepdims=False)
        within = kept.astype(jnp.float32) + lax.ppermute(sent, "fc", swap).astype(jnp.float32)
        return within.astype(jnp.bfloat16)

    def scatter_chips(within):
        return lax.psum_scatter(within, "fy", scatter_dimension=0, tiled=False)

    def to_token_layout(shares):
        returned = lax.all_to_all(
            shares.reshape(dp_count, CAP, feat),
            "dp",
            split_axis=0,
            concat_axis=0,
            tiled=True,
        ).astype(jnp.float32)
        return jnp.sum(returned.reshape(E, groups, CAP, feat), axis=1).reshape(slot_total, feat)

    gate_w3 = w_gate.reshape(fsdp_count, feat, hid)
    up_w3 = w_up.reshape(fsdp_count, feat, hid)
    down_w3 = w_down.reshape(hid, fsdp_count, feat)
    in_dims = (((0, 2), (0, 1)), ((), ()))

    expert_rows = join_cores(to_expert_layout(tokens, False))
    gate_proj = lax.dot_general(expert_rows, gate_w3, in_dims, preferred_element_type=jnp.float32)
    up_proj = lax.dot_general(expert_rows, up_w3, in_dims, preferred_element_type=jnp.float32)
    sigmoid_gate = jax.nn.sigmoid(gate_proj)
    activated = gate_proj * sigmoid_gate
    hidden = (activated * up_proj).astype(jnp.bfloat16)
    out_partial = jnp.einsum(
        "rh,hfd->frd", hidden, down_w3, preferred_element_type=jnp.float32
    )
    grad_across = to_expert_layout(out_grad, True)
    out_within, grad_across = lax.optimization_barrier((swap_cores(out_partial), grad_across))
    out_slots = to_token_layout(scatter_chips(out_within))
    first_pair = jnp.dot(
        select_first.astype(jnp.float32),
        out_slots,
        precision=lax.Precision.HIGHEST,
        preferred_element_type=jnp.float32,
    )
    second_pair = jnp.dot(
        select_second.astype(jnp.float32),
        out_slots,
        precision=lax.Precision.HIGHEST,
        preferred_element_type=jnp.float32,
    )
    mixed = (route_probs[:, 0:1] * first_pair + route_probs[:, 1:2] * second_pair).astype(
        jnp.bfloat16
    )
    grad_local = out_grad.astype(jnp.float32)
    prob_terms = jnp.stack(
        [jnp.sum(first_pair * grad_local, axis=1), jnp.sum(second_pair * grad_local, axis=1)],
        axis=1,
    )
    pair_terms = prob_terms + lax.ppermute(prob_terms, "fc", swap)
    prob_grad = jnp.sum(lax.all_gather(pair_terms, "fy", axis=0, tiled=False), axis=0)
    grad_rows = join_cores(grad_across)
    hidden_grad = lax.dot_general(grad_rows, down_w3, (((0, 2), (1, 2)), ((), ())),
                                  preferred_element_type=jnp.float32)
    gate_grad = (
        hidden_grad * up_proj * sigmoid_gate * (1.0 + gate_proj * (1.0 - sigmoid_gate))
    ).astype(jnp.bfloat16)
    up_grad = (hidden_grad * activated).astype(jnp.bfloat16)
    gate_weight_grad = jnp.einsum(
        "frd,rh->fdh", expert_rows, gate_grad, preferred_element_type=jnp.float32
    ).astype(jnp.bfloat16).reshape(fsdp_count * feat, hid)
    down_weight_grad = jnp.einsum(
        "hr,frd->hfd", hidden.T, grad_rows, preferred_element_type=jnp.float32
    ).astype(jnp.bfloat16).reshape(hid, model)
    input_partial = jnp.einsum(
        "rh,fdh->frd", gate_grad, gate_w3, preferred_element_type=jnp.float32
    )
    input_partial = input_partial + jnp.einsum(
        "rh,fdh->frd", up_grad, up_w3, preferred_element_type=jnp.float32
    )
    input_shares = scatter_chips(swap_cores(input_partial))
    prob_grad, gate_weight_grad, down_weight_grad, input_shares, up_grad_late = lax.optimization_barrier(
        (prob_grad, gate_weight_grad, down_weight_grad, input_shares, up_grad))
    up_weight_grad = jnp.einsum(
        "frd,rh->fdh", expert_rows, up_grad_late, preferred_element_type=jnp.float32
    ).astype(jnp.bfloat16).reshape(fsdp_count * feat, hid)
    input_slots = to_token_layout(input_shares)
    token_grad = jnp.dot(
        picker.astype(jnp.float32),
        input_slots,
        precision=lax.Precision.HIGHEST,
        preferred_element_type=jnp.float32,
    ).astype(jnp.bfloat16)
    return (mixed, token_grad, prob_grad, gate_weight_grad, up_weight_grad, down_weight_grad)


def solution(mesh):
    dp_size, fsdp_size = mesh.devices.shape
    cores = 2
    split = Mesh(mesh.devices.reshape(dp_size, fsdp_size // cores, cores), ("dp", "fy", "fc"))
    fs = ("fy", "fc")
    placed = (
        P("dp", fs),
        P("dp", None),
        P("dp", None),
        P(None, ("dp",) + fs),
        P(None, ("dp",) + fs),
        P(("dp",) + fs, None),
        P("dp", fs),
    )
    return jax.shard_map(
        local,
        mesh=split,
        in_specs=placed,
        out_specs=(
            P("dp", fs),
            P("dp", fs),
            P("dp", None),
            P(None, ("dp",) + fs),
            P(None, ("dp",) + fs),
            P(("dp",) + fs, None),
        ),
        check_vma=False,
    )
```

```python
import jax
import jax.numpy as jnp
from jax import lax
from jax.sharding import Mesh, PartitionSpec as P

E = 8
CAP = 40


def local(tokens, expert_ids, route_probs, w_gate, w_up, w_down, out_grad):
    dp_count = lax.axis_size("dp")
    chips = lax.axis_size("fy")
    cores = lax.axis_size("fc")
    fsdp_count = chips * cores
    groups = dp_count // E
    token_count = tokens.shape[0]
    feat = tokens.shape[1]
    model = w_down.shape[1]
    hid = w_gate.shape[1]
    slot_total = E * CAP
    rows = dp_count * CAP
    core = lax.axis_index("fc")
    swap = [(0, 1), (1, 0)]
    routing = expert_ids.reshape(-1)
    onehot = (routing[:, None] == jnp.arange(E, dtype=jnp.int32)[None, :]).astype(jnp.int32)
    pair_index = jnp.arange(routing.shape[0], dtype=jnp.int32)
    earlier = (pair_index[:, None] > pair_index[None, :]).astype(jnp.bfloat16)
    before = jnp.dot(earlier, onehot.astype(jnp.bfloat16), preferred_element_type=jnp.float32)
    position = jnp.sum(before * onehot.astype(jnp.float32), axis=1).astype(jnp.int32)
    slot_of = (routing * CAP + position).reshape(token_count, 2)
    slot_index = jnp.arange(slot_total, dtype=jnp.int32)
    select_first = slot_of[:, 0:1] == slot_index[None, :]
    select_second = slot_of[:, 1:2] == slot_index[None, :]
    picker = jnp.logical_or(select_first, select_second)
    picker_bf = picker.astype(jnp.bfloat16)
    weighted = jnp.where(select_first, route_probs[:, 0:1], 0.0) + jnp.where(
        select_second, route_probs[:, 1:2], 0.0
    )
    contract_rows = (((0,), (0,)), ((), ()))
    back_dims = (((1,), (1,)), ((), ()))

    def place_rows(source, scaled):
        if scaled:
            placed = lax.dot_general(
                weighted,
                source.astype(jnp.float32),
                contract_rows,
                precision=lax.Precision.HIGHEST,
                preferred_element_type=jnp.float32,
            )
        else:
            placed = lax.dot_general(
                picker_bf, source, contract_rows, preferred_element_type=jnp.float32
            )
        placed = placed.astype(jnp.bfloat16).reshape(E, CAP, source.shape[1])
        return jnp.repeat(placed, groups, axis=0)

    def to_expert_layout(source, scaled):
        arrived = lax.all_to_all(
            place_rows(source, scaled), "dp", split_axis=0, concat_axis=0, tiled=True
        )
        across = lax.all_gather(arrived.reshape(rows, feat), "fy", axis=0, tiled=False)
        return across

    def join_cores(across):
        both = lax.all_to_all(
            jnp.broadcast_to(across[:, None], (chips, cores, rows, feat)),
            "fc", split_axis=1, concat_axis=1, tiled=True,
        )
        return both.reshape(fsdp_count, rows, feat)

    def swap_cores(partial_value):
        blocks = partial_value.astype(jnp.bfloat16).reshape(chips, cores, rows, feat)
        kept = lax.dynamic_index_in_dim(blocks, core, axis=1, keepdims=False)
        sent = lax.dynamic_index_in_dim(blocks, 1 - core, axis=1, keepdims=False)
        within = kept.astype(jnp.float32) + lax.ppermute(sent, "fc", swap).astype(jnp.float32)
        return within.astype(jnp.bfloat16)

    def scatter_chips(within):
        return lax.psum_scatter(within, "fy", scatter_dimension=0, tiled=False)

    def to_token_layout(shares):
        returned = lax.all_to_all(
            shares.reshape(dp_count, CAP, feat),
            "dp",
            split_axis=0,
            concat_axis=0,
            tiled=True,
        ).astype(jnp.float32)
        return jnp.sum(returned.reshape(E, groups, CAP, feat), axis=1).reshape(slot_total, feat)

    gate_w3 = w_gate.reshape(fsdp_count, feat, hid)
    up_w3 = w_up.reshape(fsdp_count, feat, hid)
    down_w3 = w_down.reshape(hid, fsdp_count, feat)
    in_dims = (((0, 2), (0, 1)), ((), ()))

    expert_rows = join_cores(to_expert_layout(tokens, False))
    gate_proj = lax.dot_general(expert_rows, gate_w3, in_dims, preferred_element_type=jnp.float32)
    up_proj = lax.dot_general(expert_rows, up_w3, in_dims, preferred_element_type=jnp.float32)
    sigmoid_gate = jax.nn.sigmoid(gate_proj)
    activated = gate_proj * sigmoid_gate
    hidden = (activated * up_proj).astype(jnp.bfloat16)
    out_partial = jnp.einsum(
        "rh,hfd->frd", hidden, down_w3, preferred_element_type=jnp.float32
    )
    grad_across = to_expert_layout(out_grad, True)
    out_within, grad_across = lax.optimization_barrier((swap_cores(out_partial), grad_across))
    out_slots = to_token_layout(scatter_chips(out_within))
    first_pair = jnp.dot(
        select_first.astype(jnp.float32),
        out_slots,
        precision=lax.Precision.HIGHEST,
        preferred_element_type=jnp.float32,
    )
    second_pair = jnp.dot(
        select_second.astype(jnp.float32),
        out_slots,
        precision=lax.Precision.HIGHEST,
        preferred_element_type=jnp.float32,
    )
    mixed = (route_probs[:, 0:1] * first_pair + route_probs[:, 1:2] * second_pair).astype(
        jnp.bfloat16
    )
    grad_local = out_grad.astype(jnp.float32)
    prob_terms = jnp.stack(
        [jnp.sum(first_pair * grad_local, axis=1), jnp.sum(second_pair * grad_local, axis=1)],
        axis=1,
    )
    pair_terms = prob_terms + lax.ppermute(prob_terms, "fc", swap)
    prob_grad = jnp.sum(lax.all_gather(pair_terms, "fy", axis=0, tiled=False), axis=0)
    grad_rows = join_cores(grad_across)
    hidden_grad = lax.dot_general(grad_rows, down_w3, (((0, 2), (1, 2)), ((), ())),
                                  preferred_element_type=jnp.float32)
    gate_grad = (
        hidden_grad * up_proj * sigmoid_gate * (1.0 + gate_proj * (1.0 - sigmoid_gate))
    ).astype(jnp.bfloat16)
    up_grad = (hidden_grad * activated).astype(jnp.bfloat16)
    gate_weight_grad = jnp.einsum(
        "frd,rh->fdh", expert_rows, gate_grad, preferred_element_type=jnp.float32
    ).astype(jnp.bfloat16).reshape(fsdp_count * feat, hid)
    down_weight_grad = jnp.einsum(
        "hr,frd->hfd", hidden.T, grad_rows, preferred_element_type=jnp.float32
    ).astype(jnp.bfloat16).reshape(hid, model)
    input_partial = jnp.einsum(
        "rh,fdh->frd", gate_grad, gate_w3, preferred_element_type=jnp.float32
    )
    input_partial = input_partial + jnp.einsum(
        "rh,fdh->frd", up_grad, up_w3, preferred_element_type=jnp.float32
    )
    input_shares = scatter_chips(swap_cores(input_partial))
    prob_grad, gate_weight_grad, down_weight_grad, input_shares, up_grad_late = lax.optimization_barrier(
        (prob_grad, gate_weight_grad, down_weight_grad, input_shares, up_grad))
    up_weight_grad = jnp.einsum(
        "frd,rh->fdh", expert_rows, up_grad_late, preferred_element_type=jnp.float32
    ).astype(jnp.bfloat16).reshape(fsdp_count * feat, hid)
    input_slots = to_token_layout(input_shares)
    token_grad = jnp.dot(
        picker.astype(jnp.float32),
        input_slots,
        precision=lax.Precision.HIGHEST,
        preferred_element_type=jnp.float32,
    ).astype(jnp.bfloat16)
    return (mixed, token_grad, prob_grad, gate_weight_grad, up_weight_grad, down_weight_grad)


def solution(mesh):
    dp_size, fsdp_size = mesh.devices.shape
    cores = 2
    split = Mesh(mesh.devices.reshape(dp_size, fsdp_size // cores, cores), ("dp", "fy", "fc"))
    fs = ("fy", "fc")
    placed = (
        P("dp", fs),
        P("dp", None),
        P("dp", None),
        P(None, ("dp",) + fs),
        P(None, ("dp",) + fs),
        P(("dp",) + fs, None),
        P("dp", fs),
    )
    return jax.shard_map(
        local,
        mesh=split,
        in_specs=placed,
        out_specs=(
            P("dp", fs),
            P("dp", fs),
            P("dp", None),
            P(None, ("dp",) + fs),
            P(None, ("dp",) + fs),
            P(("dp",) + fs, None),
        ),
        check_vma=False,
    )
```

```python
import jax
import jax.numpy as jnp
from jax import lax
from jax.sharding import Mesh, PartitionSpec as P

E = 8
CAP = 40


def local(tokens, expert_ids, route_probs, w_gate, w_up, w_down, out_grad):
    dp_count = lax.axis_size("dp")
    chips = lax.axis_size("fy")
    cores = lax.axis_size("fc")
    fsdp_count = chips * cores
    groups = dp_count // E
    token_count = tokens.shape[0]
    feat = tokens.shape[1]
    model = w_down.shape[1]
    hid = w_gate.shape[1]
    slot_total = E * CAP
    rows = dp_count * CAP
    core = lax.axis_index("fc")
    swap = [(0, 1), (1, 0)]
    routing = expert_ids.reshape(-1)
    onehot = (routing[:, None] == jnp.arange(E, dtype=jnp.int32)[None, :]).astype(jnp.int32)
    pair_index = jnp.arange(routing.shape[0], dtype=jnp.int32)
    earlier = (pair_index[:, None] > pair_index[None, :]).astype(jnp.bfloat16)
    before = jnp.dot(earlier, onehot.astype(jnp.bfloat16), preferred_element_type=jnp.float32)
    position = jnp.sum(before * onehot.astype(jnp.float32), axis=1).astype(jnp.int32)
    slot_of = (routing * CAP + position).reshape(token_count, 2)
    slot_index = jnp.arange(slot_total, dtype=jnp.int32)
    select_first = slot_of[:, 0:1] == slot_index[None, :]
    select_second = slot_of[:, 1:2] == slot_index[None, :]
    picker = jnp.logical_or(select_first, select_second)
    picker_bf = picker.astype(jnp.bfloat16)
    weighted = jnp.where(select_first, route_probs[:, 0:1], 0.0) + jnp.where(
        select_second, route_probs[:, 1:2], 0.0
    )
    contract_rows = (((0,), (0,)), ((), ()))
    back_dims = (((1,), (1,)), ((), ()))

    def place_rows(source, scaled):
        if scaled:
            placed = lax.dot_general(
                weighted,
                source.astype(jnp.float32),
                contract_rows,
                precision=lax.Precision.HIGHEST,
                preferred_element_type=jnp.float32,
            )
        else:
            placed = lax.dot_general(
                picker_bf, source, contract_rows, preferred_element_type=jnp.float32
            )
        placed = placed.astype(jnp.bfloat16).reshape(E, CAP, source.shape[1])
        return jnp.repeat(placed, groups, axis=0)

    def to_expert_layout(source, scaled):
        arrived = lax.all_to_all(
            place_rows(source, scaled), "dp", split_axis=0, concat_axis=0, tiled=True
        )
        across = lax.all_gather(arrived.reshape(rows, feat), "fy", axis=0, tiled=False)
        return across

    def join_cores(across):
        both = lax.all_to_all(
            jnp.broadcast_to(across[:, None], (chips, cores, rows, feat)),
            "fc", split_axis=1, concat_axis=1, tiled=True,
        )
        return both.reshape(fsdp_count, rows, feat)

    def swap_cores(partial_value):
        blocks = partial_value.astype(jnp.bfloat16).reshape(chips, cores, rows, feat)
        kept = lax.dynamic_index_in_dim(blocks, core, axis=1, keepdims=False)
        sent = lax.dynamic_index_in_dim(blocks, 1 - core, axis=1, keepdims=False)
        within = kept.astype(jnp.float32) + lax.ppermute(sent, "fc", swap).astype(jnp.float32)
        return within.astype(jnp.bfloat16)

    def scatter_chips(within):
        return lax.psum_scatter(within, "fy", scatter_dimension=0, tiled=False)

    def to_token_layout(shares):
        returned = lax.all_to_all(
            shares.reshape(dp_count, CAP, feat),
            "dp",
            split_axis=0,
            concat_axis=0,
            tiled=True,
        ).astype(jnp.float32)
        return jnp.sum(returned.reshape(E, groups, CAP, feat), axis=1).reshape(slot_total, feat)

    gate_w3 = w_gate.reshape(fsdp_count, feat, hid)
    up_w3 = w_up.reshape(fsdp_count, feat, hid)
    down_w3 = w_down.reshape(hid, fsdp_count, feat)
    in_dims = (((0, 2), (0, 1)), ((), ()))

    expert_rows = join_cores(to_expert_layout(tokens, False))
    gate_proj = lax.dot_general(expert_rows, gate_w3, in_dims, preferred_element_type=jnp.float32)
    up_proj = lax.dot_general(expert_rows, up_w3, in_dims, preferred_element_type=jnp.float32)
    sigmoid_gate = jax.nn.sigmoid(gate_proj)
    activated = gate_proj * sigmoid_gate
    hidden = (activated * up_proj).astype(jnp.bfloat16)
    out_partial = jnp.einsum(
        "rh,hfd->frd", hidden, down_w3, preferred_element_type=jnp.float32
    )
    grad_across = to_expert_layout(out_grad, True)
    out_within, grad_across = lax.optimization_barrier((swap_cores(out_partial), grad_across))
    out_slots = to_token_layout(scatter_chips(out_within))
    first_pair = jnp.dot(
        select_first.astype(jnp.float32),
        out_slots,
        precision=lax.Precision.HIGHEST,
        preferred_element_type=jnp.float32,
    )
    second_pair = jnp.dot(
        select_second.astype(jnp.float32),
        out_slots,
        precision=lax.Precision.HIGHEST,
        preferred_element_type=jnp.float32,
    )
    mixed = (route_probs[:, 0:1] * first_pair + route_probs[:, 1:2] * second_pair).astype(
        jnp.bfloat16
    )
    grad_local = out_grad.astype(jnp.float32)
    prob_terms = jnp.stack(
        [jnp.sum(first_pair * grad_local, axis=1), jnp.sum(second_pair * grad_local, axis=1)],
        axis=1,
    )
    pair_terms = prob_terms + lax.ppermute(prob_terms, "fc", swap)
    prob_grad = jnp.sum(lax.all_gather(pair_terms, "fy", axis=0, tiled=False), axis=0)
    grad_rows = join_cores(grad_across)
    hidden_grad = lax.dot_general(grad_rows, down_w3, (((0, 2), (1, 2)), ((), ())),
                                  preferred_element_type=jnp.float32)
    gate_grad = (
        hidden_grad * up_proj * sigmoid_gate * (1.0 + gate_proj * (1.0 - sigmoid_gate))
    ).astype(jnp.bfloat16)
    up_grad = (hidden_grad * activated).astype(jnp.bfloat16)
    both_grads = jnp.einsum(
        "frd,rh->fdh", expert_rows, jnp.concatenate([gate_grad, up_grad], axis=1),
        preferred_element_type=jnp.float32,
    ).astype(jnp.bfloat16).reshape(fsdp_count * feat, 2 * hid)
    gate_weight_grad = both_grads[:, :hid]
    up_weight_grad = both_grads[:, hid:]
    down_weight_grad = jnp.einsum(
        "hr,frd->hfd", hidden.T, grad_rows, preferred_element_type=jnp.float32
    ).astype(jnp.bfloat16).reshape(hid, model)
    input_partial = jnp.einsum(
        "rh,fdh->frd", gate_grad, gate_w3, preferred_element_type=jnp.float32
    )
    input_partial = input_partial + jnp.einsum(
        "rh,fdh->frd", up_grad, up_w3, preferred_element_type=jnp.float32
    )
    input_shares = scatter_chips(swap_cores(input_partial))
    prob_grad, gate_weight_grad, up_weight_grad, down_weight_grad, input_shares = lax.optimization_barrier(
        (prob_grad, gate_weight_grad, up_weight_grad, down_weight_grad, input_shares))
    input_slots = to_token_layout(input_shares)
    token_grad = jnp.dot(
        picker.astype(jnp.float32),
        input_slots,
        precision=lax.Precision.HIGHEST,
        preferred_element_type=jnp.float32,
    ).astype(jnp.bfloat16)
    return (mixed, token_grad, prob_grad, gate_weight_grad, up_weight_grad, down_weight_grad)


def solution(mesh):
    dp_size, fsdp_size = mesh.devices.shape
    cores = 2
    split = Mesh(mesh.devices.reshape(dp_size, fsdp_size // cores, cores), ("dp", "fy", "fc"))
    fs = ("fy", "fc")
    placed = (
        P("dp", fs),
        P("dp", None),
        P("dp", None),
        P(None, ("dp",) + fs),
        P(None, ("dp",) + fs),
        P(("dp",) + fs, None),
        P("dp", fs),
    )
    return jax.shard_map(
        local,
        mesh=split,
        in_specs=placed,
        out_specs=(
            P("dp", fs),
            P("dp", fs),
            P("dp", None),
            P(None, ("dp",) + fs),
            P(None, ("dp",) + fs),
            P(("dp",) + fs, None),
        ),
        check_vma=False,
    )
```

```python
import jax
import jax.numpy as jnp
from jax import lax
from jax.sharding import Mesh, PartitionSpec as P

E = 8
CAP = 40


def local(tokens, expert_ids, route_probs, w_gate, w_up, w_down, out_grad):
    dp_count = lax.axis_size("dp")
    chips = lax.axis_size("fy")
    cores = lax.axis_size("fc")
    fsdp_count = chips * cores
    groups = dp_count // E
    token_count = tokens.shape[0]
    feat = tokens.shape[1]
    model = w_down.shape[1]
    hid = w_gate.shape[1]
    slot_total = E * CAP
    rows = dp_count * CAP
    core = lax.axis_index("fc")
    swap = [(0, 1), (1, 0)]
    routing = expert_ids.reshape(-1)
    onehot = (routing[:, None] == jnp.arange(E, dtype=jnp.int32)[None, :]).astype(jnp.int32)
    pair_index = jnp.arange(routing.shape[0], dtype=jnp.int32)
    earlier = (pair_index[:, None] > pair_index[None, :]).astype(jnp.bfloat16)
    before = jnp.dot(earlier, onehot.astype(jnp.bfloat16), preferred_element_type=jnp.float32)
    position = jnp.sum(before * onehot.astype(jnp.float32), axis=1).astype(jnp.int32)
    slot_of = (routing * CAP + position).reshape(token_count, 2)
    slot_index = jnp.arange(slot_total, dtype=jnp.int32)
    select_first = slot_of[:, 0:1] == slot_index[None, :]
    select_second = slot_of[:, 1:2] == slot_index[None, :]
    picker = jnp.logical_or(select_first, select_second)
    picker_bf = picker.astype(jnp.bfloat16)
    weighted = jnp.where(select_first, route_probs[:, 0:1], 0.0) + jnp.where(
        select_second, route_probs[:, 1:2], 0.0
    )
    contract_rows = (((0,), (0,)), ((), ()))
    back_dims = (((1,), (1,)), ((), ()))

    def place_rows(source, scaled):
        if scaled:
            placed = lax.dot_general(
                weighted,
                source.astype(jnp.float32),
                contract_rows,
                precision=lax.Precision.HIGHEST,
                preferred_element_type=jnp.float32,
            )
        else:
            placed = lax.dot_general(
                picker_bf, source, contract_rows, preferred_element_type=jnp.float32
            )
        placed = placed.astype(jnp.bfloat16).reshape(E, CAP, source.shape[1])
        return jnp.repeat(placed, groups, axis=0)

    def to_expert_layout(source, scaled):
        arrived = lax.all_to_all(
            place_rows(source, scaled), "dp", split_axis=0, concat_axis=0, tiled=True
        )
        across = lax.all_gather(arrived.reshape(rows, feat), "fy", axis=0, tiled=False)
        return across

    def join_cores(across):
        both = lax.all_to_all(
            jnp.broadcast_to(across[:, None], (chips, cores, rows, feat)),
            "fc", split_axis=1, concat_axis=1, tiled=True,
        )
        return both.reshape(fsdp_count, rows, feat)

    def swap_cores(partial_value):
        blocks = partial_value.astype(jnp.bfloat16).reshape(chips, cores, rows, feat)
        kept = lax.dynamic_index_in_dim(blocks, core, axis=1, keepdims=False)
        sent = lax.dynamic_index_in_dim(blocks, 1 - core, axis=1, keepdims=False)
        within = kept.astype(jnp.float32) + lax.ppermute(sent, "fc", swap).astype(jnp.float32)
        return within.astype(jnp.bfloat16)

    def scatter_chips(within):
        return lax.psum_scatter(within, "fy", scatter_dimension=0, tiled=False)

    def to_token_layout(shares):
        returned = lax.all_to_all(
            shares.reshape(dp_count, CAP, feat),
            "dp",
            split_axis=0,
            concat_axis=0,
            tiled=True,
        ).astype(jnp.float32)
        return jnp.sum(returned.reshape(E, groups, CAP, feat), axis=1).reshape(slot_total, feat)

    gate_w3 = w_gate.reshape(fsdp_count, feat, hid)
    up_w3 = w_up.reshape(fsdp_count, feat, hid)
    down_w3 = w_down.reshape(hid, fsdp_count, feat)
    in_dims = (((0, 2), (0, 1)), ((), ()))

    expert_rows = join_cores(to_expert_layout(tokens, False))
    gate_proj = lax.dot_general(expert_rows, gate_w3, in_dims, preferred_element_type=jnp.float32)
    up_proj = lax.dot_general(expert_rows, up_w3, in_dims, preferred_element_type=jnp.float32)
    sigmoid_gate = jax.nn.sigmoid(gate_proj)
    activated = gate_proj * sigmoid_gate
    hidden = (activated * up_proj).astype(jnp.bfloat16)
    out_partial = jnp.einsum(
        "rh,hfd->frd", hidden, down_w3, preferred_element_type=jnp.float32
    )
    grad_across = to_expert_layout(out_grad, True)
    out_within, grad_across = lax.optimization_barrier((swap_cores(out_partial), grad_across))
    out_slots = to_token_layout(scatter_chips(out_within))
    first_pair = jnp.take(out_slots, slot_of[:, 0], axis=0, mode="clip")
    second_pair = jnp.take(out_slots, slot_of[:, 1], axis=0, mode="clip")
    mixed = (route_probs[:, 0:1] * first_pair + route_probs[:, 1:2] * second_pair).astype(
        jnp.bfloat16
    )
    grad_local = out_grad.astype(jnp.float32)
    prob_terms = jnp.stack(
        [jnp.sum(first_pair * grad_local, axis=1), jnp.sum(second_pair * grad_local, axis=1)],
        axis=1,
    )
    pair_terms = prob_terms + lax.ppermute(prob_terms, "fc", swap)
    prob_grad = jnp.sum(lax.all_gather(pair_terms, "fy", axis=0, tiled=False), axis=0)
    grad_rows = join_cores(grad_across)
    hidden_grad = lax.dot_general(grad_rows, down_w3, (((0, 2), (1, 2)), ((), ())),
                                  preferred_element_type=jnp.float32)
    gate_grad = (
        hidden_grad * up_proj * sigmoid_gate * (1.0 + gate_proj * (1.0 - sigmoid_gate))
    ).astype(jnp.bfloat16)
    up_grad = (hidden_grad * activated).astype(jnp.bfloat16)
    gate_weight_grad = jnp.einsum(
        "frd,rh->fdh", expert_rows, gate_grad, preferred_element_type=jnp.float32
    ).astype(jnp.bfloat16).reshape(fsdp_count * feat, hid)
    down_weight_grad = jnp.einsum(
        "hr,frd->hfd", hidden.T, grad_rows, preferred_element_type=jnp.float32
    ).astype(jnp.bfloat16).reshape(hid, model)
    input_partial = jnp.einsum(
        "rh,fdh->frd", gate_grad, gate_w3, preferred_element_type=jnp.float32
    )
    input_partial = input_partial + jnp.einsum(
        "rh,fdh->frd", up_grad, up_w3, preferred_element_type=jnp.float32
    )
    input_shares = scatter_chips(swap_cores(input_partial))
    prob_grad, gate_weight_grad, down_weight_grad, input_shares, up_grad_late = lax.optimization_barrier(
        (prob_grad, gate_weight_grad, down_weight_grad, input_shares, up_grad))
    up_weight_grad = jnp.einsum(
        "frd,rh->fdh", expert_rows, up_grad_late, preferred_element_type=jnp.float32
    ).astype(jnp.bfloat16).reshape(fsdp_count * feat, hid)
    input_slots = to_token_layout(input_shares)
    token_grad = (jnp.take(input_slots, slot_of[:, 0], axis=0, mode="clip")
                  + jnp.take(input_slots, slot_of[:, 1], axis=0, mode="clip")).astype(jnp.bfloat16)
    return (mixed, token_grad, prob_grad, gate_weight_grad, up_weight_grad, down_weight_grad)


def solution(mesh):
    dp_size, fsdp_size = mesh.devices.shape
    cores = 2
    split = Mesh(mesh.devices.reshape(dp_size, fsdp_size // cores, cores), ("dp", "fy", "fc"))
    fs = ("fy", "fc")
    placed = (
        P("dp", fs),
        P("dp", None),
        P("dp", None),
        P(None, ("dp",) + fs),
        P(None, ("dp",) + fs),
        P(("dp",) + fs, None),
        P("dp", fs),
    )
    return jax.shard_map(
        local,
        mesh=split,
        in_specs=placed,
        out_specs=(
            P("dp", fs),
            P("dp", fs),
            P("dp", None),
            P(None, ("dp",) + fs),
            P(None, ("dp",) + fs),
            P(("dp",) + fs, None),
        ),
        check_vma=False,
    )
```
